256 devices in a mesh: grp: 8 (over z), dev: 32 (over y, x, core).
Axes of the slice: x: 4, y: 4, z: 8, core: 2. Of those that a mesh axis runs over, the one named last changes fastest.
Arguments:
- pool: bfloat16 [786432, 1024], P(('grp', 'dev'))
- nearest: float32 [786432], P(('grp', 'dev')), may hold values from 0.5 to 2.2
- center_owner: int32 [8, 256], P('grp'), may hold values from 0 to 31, as said below
- center_offset: int32 [8, 256], P('grp'), may hold values from 0 to 3071
Outputs:
- nearest_after: float32 [786432], P(('grp', 'dev'))
The draws below stay inside these ranges and needn't reach their ends.
Inputs may be any that keep to these rules, and one draw needn't show every extreme that they name: `center_owner`: in each group no more than 32 centers have the same owner, one owner has exactly 32, and the centers of a group are distinct rows.
All inputs are finite; a program needn't handle non-finite values.
Results may differ from the reference program's by a relative error of at most 0.0003.
Values may be sent and summed in bfloat16 or wider, within the bound.
No kernel may reach another device: no remote copies, remote signals or barrier semaphores. Data moves between devices by JAX's collectives and lax.ppermute only.
A program may use at most 64 MiB of HBM per device.

```python
import math
import jax
import jax.numpy as jnp
from jax import lax

D = 1024
C = 256
MOST = 32
ROWS_DEV = 3072
GROUPS = 8
POOL = 786432
N_DEV = 32


def centers_group(key):
    k_hot = jax.random.fold_in(key, 1)
    k_perm = jax.random.fold_in(key, 2)
    k_order = jax.random.fold_in(key, 3)
    k_start = jax.random.fold_in(key, 4)
    k_jitter = jax.random.fold_in(key, 5)
    hot = jax.random.randint(k_hot, (), 0, N_DEV)
    chosen = jax.random.permutation(k_perm, (N_DEV - 1) * MOST)[:C - MOST]
    other_owner = chosen // MOST
    other_owner = other_owner + (other_owner >= hot).astype(jnp.int32)
    other_rank = chosen % MOST
    owner = jnp.concatenate([jnp.full((MOST,), hot, jnp.int32), other_owner.astype(jnp.int32)])
    slot_rank = jnp.concatenate([jnp.arange(MOST, dtype=jnp.int32), other_rank.astype(jnp.int32)])
    order = jax.random.permutation(k_order, C)
    owner = owner[order]
    slot_rank = slot_rank[order]
    stride = ROWS_DEV // MOST
    starts = jax.random.randint(k_start, (N_DEV,), 0, ROWS_DEV)
    starts = jnp.where(jnp.arange(N_DEV, dtype=jnp.int32) == hot, 0, starts)
    jitter = jax.random.randint(k_jitter, (C,), 0, stride)
    is_hot = owner == hot
    jitter = jnp.where(is_hot & (slot_rank == MOST - 1), stride - 1, jitter)
    jitter = jnp.where(is_hot & (slot_rank == 0), 0, jitter)
    offset = (starts[owner] + slot_rank * stride + jitter) % ROWS_DEV
    return (owner.astype(jnp.int32), offset.astype(jnp.int32))


def centers_all(key):
    base = jax.random.fold_in(key, 4242)
    group_keys = jax.random.split(base, GROUPS)
    return jax.vmap(centers_group)(group_keys)


def draw_center_owner(key, part):
    return centers_all(key)[0]


def draw_center_offset(key, part):
    return centers_all(key)[1]


def draw_pool(key, part):
    k_proto = jax.random.fold_in(key, 11)
    k_ident = jax.random.fold_in(key, 12)
    k_noise = jax.random.fold_in(key, 13)
    protos = jax.random.normal(k_proto, (2 * C, D), jnp.float32)
    ident = jax.random.randint(k_ident, (POOL,), 0, 2 * C)
    noise = jax.random.normal(k_noise, (POOL, D), jnp.float32)
    values = (0.8 * protos[ident] + 0.6 * noise) / jnp.sqrt(jnp.float32(D))
    return values.astype(jnp.bfloat16)


def block_levels(rng, shape, pieces, smallest, largest):
    loudness = 1.0
    for dim, blocks in pieces:
        draws = jax.random.uniform(jax.random.fold_in(jax.random.fold_in(rng, 6), dim), (blocks,), jnp.float32, smallest / len(pieces), largest / len(pieces))
        loudness = loudness * jnp.repeat(jnp.exp(draws), shape[dim] // blocks).reshape((-1,) + (1,) * (len(shape) - 1 - dim))
    return loudness


def setup_inputs(seed: int = 0) -> dict:
    splits = jax.random.split(jax.random.key(seed), 5)
    pool = draw_pool(jax.random.fold_in(splits[4], 71), 0)
    nearest = jnp.clip(0.5 + 1.7 * jax.random.uniform(splits[1], (POOL,), jnp.float32) ** block_levels(splits[1], (POOL,), ((0, 256),), -0.2, 0.2), 0.5, 2.2)
    center_owner = draw_center_owner(jax.random.fold_in(splits[4], 71), 0)
    center_offset = draw_center_offset(jax.random.fold_in(splits[4], 71), 0)
    return dict(pool=pool, nearest=nearest, center_owner=center_owner, center_offset=center_offset)


def reference(pool, nearest, center_owner, center_offset):
    group_base = (jnp.arange(GROUPS, dtype=jnp.int32) * (N_DEV * ROWS_DEV))[:, None]
    index = (group_base + center_owner * ROWS_DEV + center_offset).reshape(-1).astype(jnp.int32)
    union = jnp.take(pool, index, axis=0)
    wide_union = union.astype(jnp.float32)
    center_norm = jnp.sum(wide_union * wide_union, axis=1)
    block = math.gcd(ROWS_DEV, 512)
    blocks = POOL // block

    def one_block(args):
        block_rows, block_near = args
        wide_rows = block_rows.astype(jnp.float32)
        row_norm = jnp.sum(wide_rows * wide_rows, axis=1)
        inner = jnp.dot(block_rows, union.T, preferred_element_type=jnp.float32)
        distance = jnp.maximum(row_norm[:, None] + center_norm[None, :] - 2.0 * inner, 0.0)
        return jnp.minimum(block_near, jnp.min(distance, axis=1))

    result = lax.map(one_block, (pool.reshape(blocks, block, D), nearest.reshape(blocks, block)))
    return result.reshape(POOL)
```

```python
import math

import jax
import jax.numpy as jnp
from jax import lax
from jax.sharding import PartitionSpec as P

MOST = 32
X_CHIPS = 4
CORES = 2


def fold_chunk(pool_rows, row_norm, running, fragment):
    center_norm = jnp.einsum("cd,cd->c", fragment, fragment, preferred_element_type=jnp.float32)
    total_rows = pool_rows.shape[0]
    block = math.gcd(total_rows, 512)
    blocks = total_rows // block

    def one_block(args):
        block_rows, block_norm, block_near = args
        inner = lax.dot_general(
            block_rows, fragment, (((1,), (1,)), ((), ())), preferred_element_type=jnp.float32
        )
        distance = jnp.maximum(block_norm[:, None] + center_norm[None, :] - 2.0 * inner, 0.0)
        return jnp.minimum(block_near, jnp.min(distance, axis=1))

    result = lax.map(
        one_block,
        (
            pool_rows.reshape(blocks, block, pool_rows.shape[1]),
            row_norm.reshape(blocks, block),
            running.reshape(blocks, block),
        ),
    )
    return result.reshape(total_rows)


def x_step(d, s, dev_count):
    chips = dev_count // CORES
    y, rest = divmod(d, X_CHIPS * CORES)
    x, c = divmod(rest, CORES)
    del chips
    return (y * X_CHIPS + (x + s) % X_CHIPS) * CORES + c


def y_step(d, s, dev_count):
    ys = dev_count // (X_CHIPS * CORES)
    y, rest = divmod(d, X_CHIPS * CORES)
    return ((y + s) % ys) * X_CHIPS * CORES + rest


def ring_gather(block, send):
    n = send.size
    got = [block]
    fwd = block
    bwd = block
    steps = (n - 1) // 2
    for _ in range(steps):
        fwd = send(fwd, 1)
        bwd = send(bwd, -1)
        got += [fwd, bwd]
    if n % 2 == 0:
        fwd = send(fwd, 1)
        got.append(fwd)
    return got


class Ring:
    def __init__(self, size, fn):
        self.size = size
        self.fn = fn

    def __call__(self, x, s):
        return self.fn(x, s)


def shards(pool, nearest, center_owner, center_offset):
    owners = center_owner[0]
    offsets = center_offset[0]
    dev_count = lax.axis_size("dev")
    grp_count = lax.axis_size("grp")
    my_index = lax.axis_index("dev")
    per_device = owners.shape[0] // dev_count

    with jax.named_scope("compact_centers"):
        send_rows = jnp.take(pool, jnp.where(owners == my_index, offsets, 0), axis=0)
        landed = lax.all_to_all(send_rows, "dev", 0, 0, tiled=True)
        mine = lax.dynamic_slice_in_dim(owners, my_index * per_device, per_device)
        compact = jnp.take(
            landed, mine * per_device + jnp.arange(per_device, dtype=jnp.int32), axis=0
        )

    def z_send(x, s):
        return lax.ppermute(x, "grp", [(g, (g + s) % grp_count) for g in range(grp_count)])

    def x_send(x, s):
        return lax.ppermute(x, "dev", [(d, x_step(d, s, dev_count)) for d in range(dev_count)])

    def y_send(x, s):
        return lax.ppermute(x, "dev", [(d, y_step(d, s, dev_count)) for d in range(dev_count)])

    y_count = dev_count // (X_CHIPS * CORES)
    row_norm = jnp.einsum("rd,rd->r", pool, pool, preferred_element_type=jnp.float32)

    with jax.named_scope("spread_centers"):
        z_all = jnp.concatenate(ring_gather(compact, Ring(grp_count, z_send)), axis=0)
        x_all = jnp.concatenate(ring_gather(z_all, Ring(X_CHIPS, x_send)), axis=0)
        y_parts = ring_gather(x_all, Ring(y_count, y_send))
        half = jnp.concatenate(y_parts, axis=0)
        other = lax.ppermute(half, "dev", [(d, d ^ 1) for d in range(dev_count)])

    with jax.named_scope("distance_min"):
        running = nearest
        for part in y_parts:
            running = fold_chunk(pool, row_norm, running, part)
        running = fold_chunk(pool, row_norm, running, other)
    return running


def solution(mesh):
    in_specs = (P(("grp", "dev"), None), P(("grp", "dev")), P("grp", None), P("grp", None))
    out_specs = P(("grp", "dev"))
    return jax.shard_map(shards, mesh=mesh, in_specs=in_specs, out_specs=out_specs, check_vma=False)
```

```python
import math

import jax
import jax.numpy as jnp
from jax import lax
from jax.sharding import PartitionSpec as P

MOST = 32
X_CHIPS = 4
CORES = 2


def fold_chunk(pool_rows, row_norm, running, fragment):
    center_norm = jnp.einsum("cd,cd->c", fragment, fragment, preferred_element_type=jnp.float32)
    total_rows = pool_rows.shape[0]
    block = math.gcd(total_rows, 512)
    blocks = total_rows // block

    def one_block(args):
        block_rows, block_norm, block_near = args
        inner = lax.dot_general(
            block_rows, fragment, (((1,), (1,)), ((), ())), preferred_element_type=jnp.float32
        )
        distance = jnp.maximum(block_norm[:, None] + center_norm[None, :] - 2.0 * inner, 0.0)
        return jnp.minimum(block_near, jnp.min(distance, axis=1))

    result = lax.map(
        one_block,
        (
            pool_rows.reshape(blocks, block, pool_rows.shape[1]),
            row_norm.reshape(blocks, block),
            running.reshape(blocks, block),
        ),
    )
    return result.reshape(total_rows)


def x_step(d, s, dev_count):
    chips = dev_count // CORES
    y, rest = divmod(d, X_CHIPS * CORES)
    x, c = divmod(rest, CORES)
    del chips
    return (y * X_CHIPS + (x + s) % X_CHIPS) * CORES + c


def y_step(d, s, dev_count):
    ys = dev_count // (X_CHIPS * CORES)
    y, rest = divmod(d, X_CHIPS * CORES)
    return ((y + s) % ys) * X_CHIPS * CORES + rest


def ring_gather(block, send):
    n = send.size
    got = [block]
    fwd = block
    bwd = block
    steps = (n - 1) // 2
    for _ in range(steps):
        fwd = send(fwd, 1)
        bwd = send(bwd, -1)
        got += [fwd, bwd]
    if n % 2 == 0:
        fwd = send(fwd, 1)
        got.append(fwd)
    return got


class Ring:
    def __init__(self, size, fn):
        self.size = size
        self.fn = fn

    def __call__(self, x, s):
        return self.fn(x, s)


def shards(pool, nearest, center_owner, center_offset):
    owners = center_owner[0]
    offsets = center_offset[0]
    dev_count = lax.axis_size("dev")
    grp_count = lax.axis_size("grp")
    my_index = lax.axis_index("dev")
    per_device = owners.shape[0] // dev_count

    with jax.named_scope("compact_centers"):
        send_rows = jnp.take(pool, jnp.where(owners == my_index, offsets, 0), axis=0)
        landed = lax.all_to_all(send_rows, "dev", 0, 0, tiled=True)
        mine = lax.dynamic_slice_in_dim(owners, my_index * per_device, per_device)
        compact = jnp.take(
            landed, mine * per_device + jnp.arange(per_device, dtype=jnp.int32), axis=0
        )

    def z_send(x, s):
        return lax.ppermute(x, "grp", [(g, (g + s) % grp_count) for g in range(grp_count)])

    def x_send(x, s):
        return lax.ppermute(x, "dev", [(d, x_step(d, s, dev_count)) for d in range(dev_count)])

    def y_send(x, s):
        return lax.ppermute(x, "dev", [(d, y_step(d, s, dev_count)) for d in range(dev_count)])

    y_count = dev_count // (X_CHIPS * CORES)
    row_norm = jnp.einsum("rd,rd->r", pool, pool, preferred_element_type=jnp.float32)

    with jax.named_scope("spread_centers"):
        z_all = jnp.concatenate(
            [compact] + [z_send(compact, s) for s in range(1, grp_count)], axis=0
        )
        x_all = jnp.concatenate(
            [z_all] + [x_send(z_all, s) for s in range(1, X_CHIPS)], axis=0
        )
        half = jnp.concatenate(ring_gather(x_all, Ring(y_count, y_send)), axis=0)
        other = lax.ppermute(half, "dev", [(d, d ^ 1) for d in range(dev_count)])

    with jax.named_scope("distance_min"):
        running = fold_chunk(pool, row_norm, nearest, half)
        running = fold_chunk(pool, row_norm, running, other)
    return running


def solution(mesh):
    in_specs = (P(("grp", "dev"), None), P(("grp", "dev")), P("grp", None), P("grp", None))
    out_specs = P(("grp", "dev"))
    return jax.shard_map(shards, mesh=mesh, in_specs=in_specs, out_specs=out_specs, check_vma=False)
```

```python
import math

import jax
import jax.numpy as jnp
from jax import lax
from jax.sharding import Mesh, PartitionSpec as P

MOST = 32
X_CHIPS = 4
CORES = 2


def fold_chunk(pool_rows, row_norm, running, fragment):
    center_norm = jnp.einsum("cd,cd->c", fragment, fragment, preferred_element_type=jnp.float32)
    total_rows = pool_rows.shape[0]
    block = total_rows
    blocks = total_rows // block

    def one_block(args):
        block_rows, block_norm, block_near = args
        inner = lax.dot_general(
            block_rows, fragment, (((1,), (1,)), ((), ())), preferred_element_type=jnp.float32
        )
        distance = jnp.maximum(block_norm[:, None] + center_norm[None, :] - 2.0 * inner, 0.0)
        return jnp.minimum(block_near, jnp.min(distance, axis=1))

    result = lax.map(
        one_block,
        (
            pool_rows.reshape(blocks, block, pool_rows.shape[1]),
            row_norm.reshape(blocks, block),
            running.reshape(blocks, block),
        ),
    )
    return result.reshape(total_rows)


def ring_gather(block, send, size):
    got = [block]
    fwd = block
    bwd = block
    for _ in range((size - 1) // 2):
        fwd = send(fwd, 1)
        bwd = send(bwd, -1)
        got += [fwd, bwd]
    if size % 2 == 0:
        fwd = send(fwd, 1)
        got.append(fwd)
    return got


def replicate_gather(x, axes, count):
    copies = jnp.broadcast_to(x[None], (count,) + x.shape)
    got = lax.all_to_all(copies, axes, 0, 0, tiled=True)
    return got.reshape((count * x.shape[0],) + x.shape[1:])


DEV_AXES = ("y", "x", "c")


def shards(pool, nearest, center_owner, center_offset):
    owners = center_owner[0]
    offsets = center_offset[0]
    dev_count = lax.axis_size(DEV_AXES)
    z_count = lax.axis_size("z")
    x_count = lax.axis_size("x")
    y_count = lax.axis_size("y")
    my_index = lax.axis_index(DEV_AXES)
    per_device = owners.shape[0] // dev_count

    with jax.named_scope("compact_centers"):
        send_rows = jnp.take(pool, jnp.where(owners == my_index, offsets, 0), axis=0)
        landed = lax.all_to_all(send_rows, DEV_AXES, 0, 0, tiled=True)
        mine = lax.dynamic_slice_in_dim(owners, my_index * per_device, per_device)
        compact = jnp.take(
            landed, mine * per_device + jnp.arange(per_device, dtype=jnp.int32), axis=0
        )

    def y_send(x, s):
        return lax.ppermute(x, "y", [(i, (i + s) % y_count) for i in range(y_count)])

    row_norm = jnp.einsum("rd,rd->r", pool, pool, preferred_element_type=jnp.float32)

    with jax.named_scope("spread_centers"):
        z_all = replicate_gather(compact, "z", z_count)
        x_all = replicate_gather(z_all, "x", x_count)
        half = jnp.concatenate(ring_gather(x_all, y_send, y_count), axis=0)
        other = lax.ppermute(half, "c", [(0, 1), (1, 0)])

    with jax.named_scope("distance_min"):
        running = fold_chunk(pool, row_norm, nearest, half)
        running = fold_chunk(pool, row_norm, running, other)
    return running


def solution(mesh):
    grp_count = mesh.shape["grp"]
    dev_count = mesh.shape["dev"]
    y_count = dev_count // (X_CHIPS * CORES)
    torus = Mesh(mesh.devices.reshape(grp_count, y_count, X_CHIPS, CORES), ("z",) + DEV_AXES)
    rows = ("z",) + DEV_AXES
    in_specs = (P(rows, None), P(rows), P("z", None), P("z", None))
    out_specs = P(rows)
    return jax.shard_map(shards, mesh=torus, in_specs=in_specs, out_specs=out_specs, check_vma=False)
```

```python
import math

import jax
import jax.numpy as jnp
from jax import lax
from jax.sharding import Mesh, PartitionSpec as P

MOST = 32
X_CHIPS = 4
CORES = 2


def fold_chunk(pool_rows, row_norm, running, fragment):
    center_norm = jnp.einsum("cd,cd->c", fragment, fragment, preferred_element_type=jnp.float32)
    total_rows = pool_rows.shape[0]
    block = total_rows
    blocks = total_rows // block

    def one_block(args):
        block_rows, block_norm, block_near = args
        inner = lax.dot_general(
            block_rows, fragment, (((1,), (1,)), ((), ())), preferred_element_type=jnp.float32
        )
        distance = jnp.maximum(block_norm[:, None] + center_norm[None, :] - 2.0 * inner, 0.0)
        return jnp.minimum(block_near, jnp.min(distance, axis=1))

    result = lax.map(
        one_block,
        (
            pool_rows.reshape(blocks, block, pool_rows.shape[1]),
            row_norm.reshape(blocks, block),
            running.reshape(blocks, block),
        ),
    )
    return result.reshape(total_rows)


def ring_gather(block, send, size):
    got = [block]
    fwd = block
    bwd = block
    for _ in range((size - 1) // 2):
        fwd = send(fwd, 1)
        bwd = send(bwd, -1)
        got += [fwd, bwd]
    if size % 2 == 0:
        fwd = send(fwd, 1)
        got.append(fwd)
    return got


def replicate_gather(x, axes, count):
    copies = jnp.broadcast_to(x[None], (count,) + x.shape)
    got = lax.all_to_all(copies, axes, 0, 0, tiled=True)
    return got.reshape((count * x.shape[0],) + x.shape[1:])


DEV_AXES = ("y", "x", "c")


def shards(pool, nearest, center_owner, center_offset):
    owners = center_owner[0]
    offsets = center_offset[0]
    dev_count = lax.axis_size(DEV_AXES)
    z_count = lax.axis_size("z")
    x_count = lax.axis_size("x")
    y_count = lax.axis_size("y")
    my_index = lax.axis_index(DEV_AXES)
    per_device = owners.shape[0] // dev_count

    with jax.named_scope("compact_centers"):
        send_rows = jnp.take(pool, jnp.where(owners == my_index, offsets, 0), axis=0)
        landed = lax.all_to_all(send_rows, DEV_AXES, 0, 0, tiled=True)
        mine = lax.dynamic_slice_in_dim(owners, my_index * per_device, per_device)
        compact = jnp.take(
            landed, mine * per_device + jnp.arange(per_device, dtype=jnp.int32), axis=0
        )

    def y_send(x, s):
        return lax.ppermute(x, "y", [(i, (i + s) % y_count) for i in range(y_count)])

    row_norm = jnp.einsum("rd,rd->r", pool, pool, preferred_element_type=jnp.float32)

    def core_swap(x):
        return lax.ppermute(x, "c", [(0, 1), (1, 0)])

    with jax.named_scope("spread_centers"):
        plane = replicate_gather(compact, ("z", "x"), z_count * x_count)
        y_near = y_send(plane, 1), y_send(plane, -1)
        y_far = y_send(y_near[0], 1)
        near = jnp.concatenate(y_near, axis=0)
        pieces = [plane, core_swap(plane), near, core_swap(near), y_far, core_swap(y_far)]

    with jax.named_scope("distance_min"):
        running = nearest
        for piece in pieces:
            running = fold_chunk(pool, row_norm, running, piece)
    return running


def solution(mesh):
    grp_count = mesh.shape["grp"]
    dev_count = mesh.shape["dev"]
    y_count = dev_count // (X_CHIPS * CORES)
    torus = Mesh(mesh.devices.reshape(grp_count, y_count, X_CHIPS, CORES), ("z",) + DEV_AXES)
    rows = ("z",) + DEV_AXES
    in_specs = (P(rows, None), P(rows), P("z", None), P("z", None))
    out_specs = P(rows)
    return jax.shard_map(shards, mesh=torus, in_specs=in_specs, out_specs=out_specs, check_vma=False)
```

```python
import math

import jax
import jax.numpy as jnp
from jax import lax
from jax.sharding import Mesh, PartitionSpec as P

MOST = 32
X_CHIPS = 4
CORES = 2


def fold_chunk(pool_rows, row_norm, running, fragment):
    center_norm = jnp.einsum("cd,cd->c", fragment, fragment, preferred_element_type=jnp.float32)
    total_rows = pool_rows.shape[0]
    block = total_rows
    blocks = total_rows // block

    def one_block(args):
        block_rows, block_norm, block_near = args
        inner = lax.dot_general(
            block_rows, fragment, (((1,), (1,)), ((), ())), preferred_element_type=jnp.float32
        )
        distance = jnp.maximum(block_norm[:, None] + center_norm[None, :] - 2.0 * inner, 0.0)
        return jnp.minimum(block_near, jnp.min(distance, axis=1))

    result = lax.map(
        one_block,
        (
            pool_rows.reshape(blocks, block, pool_rows.shape[1]),
            row_norm.reshape(blocks, block),
            running.reshape(blocks, block),
        ),
    )
    return result.reshape(total_rows)


def ring_gather(block, send, size):
    got = [block]
    fwd = block
    bwd = block
    for _ in range((size - 1) // 2):
        fwd = send(fwd, 1)
        bwd = send(bwd, -1)
        got += [fwd, bwd]
    if size % 2 == 0:
        fwd = send(fwd, 1)
        got.append(fwd)
    return got


def replicate_gather(x, axes, count):
    copies = jnp.broadcast_to(x[None], (count,) + x.shape)
    got = lax.all_to_all(copies, axes, 0, 0, tiled=True)
    return got.reshape((count * x.shape[0],) + x.shape[1:])


DEV_AXES = ("y", "x", "c")


def shards(pool, nearest, center_owner, center_offset):
    owners = center_owner[0]
    offsets = center_offset[0]
    dev_count = lax.axis_size(DEV_AXES)
    z_count = lax.axis_size("z")
    x_count = lax.axis_size("x")
    y_count = lax.axis_size("y")
    my_index = lax.axis_index(DEV_AXES)
    per_device = owners.shape[0] // dev_count

    with jax.named_scope("compact_centers"):
        devices = jnp.arange(dev_count, dtype=jnp.int32)
        owner_hot = (owners[:, None] == devices[None, :]).astype(jnp.int32)
        counts = jnp.sum(owner_hot, axis=0)
        ends = jnp.cumsum(counts)
        rank = jnp.sum((jnp.cumsum(owner_hot, axis=0) - 1) * owner_hot, axis=1)
        position = ends[owners] - counts[owners] + rank
        to_peer = ((owners == my_index)[None, :]) & (
            (position % dev_count)[None, :] == devices[:, None]
        )
        peer_offset = jnp.sum(jnp.where(to_peer, offsets[None, :], 0), axis=1)
        peer_valid = jnp.any(to_peer, axis=1)
        rows_iota = lax.broadcasted_iota(jnp.int32, (dev_count, pool.shape[0]), 1)
        pick = ((rows_iota == peer_offset[:, None]) & peer_valid[:, None]).astype(pool.dtype)
        send_rows = jnp.dot(pick, pool, preferred_element_type=jnp.float32).astype(pool.dtype)
        landed = lax.all_to_all(send_rows, DEV_AXES, 0, 0, tiled=True)
        wanted = my_index + dev_count * jnp.arange(per_device, dtype=jnp.int32)
        source = jnp.sum((ends[None, :] <= wanted[:, None]).astype(jnp.int32), axis=1)
        compact = jnp.take(landed, source, axis=0)

    def y_send(x, s):
        return lax.ppermute(x, "y", [(i, (i + s) % y_count) for i in range(y_count)])

    row_norm = jnp.einsum("rd,rd->r", pool, pool, preferred_element_type=jnp.float32)

    def core_swap(x):
        return lax.ppermute(x, "c", [(0, 1), (1, 0)])

    with jax.named_scope("spread_centers"):
        plane = replicate_gather(compact, ("z", "x"), z_count * x_count)
        y_near = y_send(plane, 1), y_send(plane, -1)
        y_far = y_send(y_near[0], 1)
        near = jnp.concatenate(y_near, axis=0)
        pieces = [plane, core_swap(plane), near, core_swap(near), y_far, core_swap(y_far)]

    with jax.named_scope("distance_min"):
        running = nearest
        for piece in pieces:
            running = fold_chunk(pool, row_norm, running, piece)
    return running


def solution(mesh):
    grp_count = mesh.shape["grp"]
    dev_count = mesh.shape["dev"]
    y_count = dev_count // (X_CHIPS * CORES)
    torus = Mesh(mesh.devices.reshape(grp_count, y_count, X_CHIPS, CORES), ("z",) + DEV_AXES)
    rows = ("z",) + DEV_AXES
    in_specs = (P(rows, None), P(rows), P("z", None), P("z", None))
    out_specs = P(rows)
    return jax.shard_map(shards, mesh=torus, in_specs=in_specs, out_specs=out_specs, check_vma=False)
```

```python
import math

import jax
import jax.numpy as jnp
from jax import lax
from jax.sharding import Mesh, PartitionSpec as P

MOST = 32
X_CHIPS = 4
CORES = 2


def fold_chunk(pool_rows, row_norm, running, fragment):
    center_norm = jnp.einsum("cd,cd->c", fragment, fragment, preferred_element_type=jnp.float32)
    total_rows = pool_rows.shape[0]
    block = total_rows
    blocks = total_rows // block

    def one_block(args):
        block_rows, block_norm, block_near = args
        inner = lax.dot_general(
            block_rows, fragment, (((1,), (1,)), ((), ())), preferred_element_type=jnp.float32
        )
        distance = jnp.maximum(block_norm[:, None] + center_norm[None, :] - 2.0 * inner, 0.0)
        return jnp.minimum(block_near, jnp.min(distance, axis=1))

    result = lax.map(
        one_block,
        (
            pool_rows.reshape(blocks, block, pool_rows.shape[1]),
            row_norm.reshape(blocks, block),
            running.reshape(blocks, block),
        ),
    )
    return result.reshape(total_rows)


def ring_gather(block, send, size):
    got = [block]
    fwd = block
    bwd = block
    for _ in range((size - 1) // 2):
        fwd = send(fwd, 1)
        bwd = send(bwd, -1)
        got += [fwd, bwd]
    if size % 2 == 0:
        fwd = send(fwd, 1)
        got.append(fwd)
    return got


def replicate_gather(x, axes, count):
    copies = jnp.broadcast_to(x[None], (count,) + x.shape)
    got = lax.all_to_all(copies, axes, 0, 0, tiled=True)
    return got.reshape((count * x.shape[0],) + x.shape[1:])


DEV_AXES = ("y", "x", "c")


def shards(pool, nearest, center_owner, center_offset):
    owners = center_owner[0]
    offsets = center_offset[0]
    dev_count = lax.axis_size(DEV_AXES)
    z_count = lax.axis_size("z")
    x_count = lax.axis_size("x")
    y_count = lax.axis_size("y")
    my_index = lax.axis_index(DEV_AXES)
    per_device = owners.shape[0] // dev_count

    with jax.named_scope("compact_centers"):
        devices = jnp.arange(dev_count, dtype=jnp.int32)
        owner_hot = (owners[:, None] == devices[None, :]).astype(jnp.int32)
        counts = jnp.sum(owner_hot, axis=0)
        ends = jnp.cumsum(counts)
        rank = jnp.sum((jnp.cumsum(owner_hot, axis=0) - 1) * owner_hot, axis=1)
        starts = jnp.sum(owner_hot * (ends - counts)[None, :], axis=1)
        position = starts + rank
        to_peer = ((owners == my_index)[None, :]) & (
            (position % dev_count)[None, :] == devices[:, None]
        )
        peer_offset = jnp.sum(jnp.where(to_peer, offsets[None, :], 0), axis=1)
        send_rows = jnp.take(pool, peer_offset, axis=0)
        landed = lax.all_to_all(send_rows, DEV_AXES, 0, 0, tiled=True)
        wanted = my_index + dev_count * jnp.arange(per_device, dtype=jnp.int32)
        source = jnp.sum((ends[None, :] <= wanted[:, None]).astype(jnp.int32), axis=1)
        compact = jnp.take(landed, source, axis=0)

    def y_send(x, s):
        return lax.ppermute(x, "y", [(i, (i + s) % y_count) for i in range(y_count)])

    row_norm = jnp.einsum("rd,rd->r", pool, pool, preferred_element_type=jnp.float32)

    def core_swap(x):
        return lax.ppermute(x, "c", [(0, 1), (1, 0)])

    with jax.named_scope("spread_centers"):
        plane = replicate_gather(compact, ("z", "x"), z_count * x_count)
        y_near = y_send(plane, 1), y_send(plane, -1)
        y_far = y_send(y_near[0], 1)
        near = jnp.concatenate(y_near, axis=0)
        pieces = [plane, core_swap(plane), near, core_swap(near), y_far, core_swap(y_far)]

    with jax.named_scope("distance_min"):
        running = nearest
        for piece in pieces:
            running = fold_chunk(pool, row_norm, running, piece)
    return running


def solution(mesh):
    grp_count = mesh.shape["grp"]
    dev_count = mesh.shape["dev"]
    y_count = dev_count // (X_CHIPS * CORES)
    torus = Mesh(mesh.devices.reshape(grp_count, y_count, X_CHIPS, CORES), ("z",) + DEV_AXES)
    rows = ("z",) + DEV_AXES
    in_specs = (P(rows, None), P(rows), P("z", None), P("z", None))
    out_specs = P(rows)
    return jax.shard_map(shards, mesh=torus, in_specs=in_specs, out_specs=out_specs, check_vma=False)
```

```python
import math

import jax
import jax.numpy as jnp
from jax import lax
from jax.sharding import Mesh, PartitionSpec as P

MOST = 32
X_CHIPS = 4
CORES = 2


def fold_chunk(pool_rows, row_norm, running, fragment):
    center_norm = jnp.einsum("cd,cd->c", fragment, fragment, preferred_element_type=jnp.float32)
    total_rows = pool_rows.shape[0]
    block = total_rows
    blocks = total_rows // block

    def one_block(args):
        block_rows, block_norm, block_near = args
        inner = lax.dot_general(
            block_rows, fragment, (((1,), (1,)), ((), ())), preferred_element_type=jnp.float32
        )
        distance = jnp.maximum(block_norm[:, None] + center_norm[None, :] - 2.0 * inner, 0.0)
        return jnp.minimum(block_near, jnp.min(distance, axis=1))

    result = lax.map(
        one_block,
        (
            pool_rows.reshape(blocks, block, pool_rows.shape[1]),
            row_norm.reshape(blocks, block),
            running.reshape(blocks, block),
        ),
    )
    return result.reshape(total_rows)


def ring_gather(block, send, size):
    got = [block]
    fwd = block
    bwd = block
    for _ in range((size - 1) // 2):
        fwd = send(fwd, 1)
        bwd = send(bwd, -1)
        got += [fwd, bwd]
    if size % 2 == 0:
        fwd = send(fwd, 1)
        got.append(fwd)
    return got


def replicate_gather(x, axes, count):
    copies = jnp.broadcast_to(x[None], (count,) + x.shape)
    got = lax.all_to_all(copies, axes, 0, 0, tiled=True)
    return got.reshape((count * x.shape[0],) + x.shape[1:])


DEV_AXES = ("y", "x", "c")


def shards(pool, nearest, center_owner, center_offset):
    owners = center_owner[0]
    offsets = center_offset[0]
    dev_count = lax.axis_size(DEV_AXES)
    z_count = lax.axis_size("z")
    x_count = lax.axis_size("x")
    y_count = lax.axis_size("y")
    my_index = lax.axis_index(DEV_AXES)
    per_device = owners.shape[0] // dev_count

    with jax.named_scope("compact_centers"):
        devices = jnp.arange(dev_count, dtype=jnp.int32)
        center_count = owners.shape[0]
        key = owners * center_count + jnp.arange(center_count, dtype=jnp.int32)
        position = jnp.sum((key[None, :] < key[:, None]).astype(jnp.int32), axis=1)
        to_peer = ((owners == my_index)[None, :]) & (
            (position % dev_count)[None, :] == devices[:, None]
        )
        peer_offset = jnp.sum(jnp.where(to_peer, offsets[None, :], 0), axis=1)
        send_rows = jnp.take(pool, peer_offset, axis=0)
        landed = lax.all_to_all(send_rows, DEV_AXES, 0, 0, tiled=True)
        wanted = my_index + dev_count * jnp.arange(per_device, dtype=jnp.int32)
        source = jnp.sum(
            jnp.where(position[None, :] == wanted[:, None], owners[None, :], 0), axis=1
        )
        compact = jnp.take(landed, source, axis=0)

    def y_send(x, s):
        return lax.ppermute(x, "y", [(i, (i + s) % y_count) for i in range(y_count)])

    row_norm = jnp.einsum("rd,rd->r", pool, pool, preferred_element_type=jnp.float32)

    def core_swap(x):
        return lax.ppermute(x, "c", [(0, 1), (1, 0)])

    with jax.named_scope("spread_centers"):
        plane = replicate_gather(compact, ("z", "x"), z_count * x_count)
        y_near = y_send(plane, 1), y_send(plane, -1)
        split = plane.shape[0] // 2
        y_far = jnp.concatenate(
            [y_send(y_near[0][:split], 1), y_send(y_near[1][split:], -1)], axis=0
        )
        near = jnp.concatenate(y_near, axis=0)
        pieces = [plane, core_swap(plane), near, core_swap(near), y_far, core_swap(y_far)]

    with jax.named_scope("distance_min"):
        running = nearest
        for piece in pieces:
            running = fold_chunk(pool, row_norm, running, piece)
    return running


def solution(mesh):
    grp_count = mesh.shape["grp"]
    dev_count = mesh.shape["dev"]
    y_count = dev_count // (X_CHIPS * CORES)
    torus = Mesh(mesh.devices.reshape(grp_count, y_count, X_CHIPS, CORES), ("z",) + DEV_AXES)
    rows = ("z",) + DEV_AXES
    in_specs = (P(rows, None), P(rows), P("z", None), P("z", None))
    out_specs = P(rows)
    return jax.shard_map(shards, mesh=torus, in_specs=in_specs, out_specs=out_specs, check_vma=False)
```

```python
import math

import jax
import jax.numpy as jnp
from jax import lax
from jax.sharding import Mesh, PartitionSpec as P

MOST = 32
X_CHIPS = 4
CORES = 2


def fold_chunk(pool_rows, row_norm, running, fragment):
    center_norm = jnp.einsum("cd,cd->c", fragment, fragment, preferred_element_type=jnp.float32)
    total_rows = pool_rows.shape[0]
    block = total_rows
    blocks = total_rows // block

    def one_block(args):
        block_rows, block_norm, block_near = args
        inner = lax.dot_general(
            block_rows, fragment, (((1,), (1,)), ((), ())), preferred_element_type=jnp.float32
        )
        distance = jnp.maximum(block_norm[:, None] + center_norm[None, :] - 2.0 * inner, 0.0)
        return jnp.minimum(block_near, jnp.min(distance, axis=1))

    result = lax.map(
        one_block,
        (
            pool_rows.reshape(blocks, block, pool_rows.shape[1]),
            row_norm.reshape(blocks, block),
            running.reshape(blocks, block),
        ),
    )
    return result.reshape(total_rows)


def ring_gather(block, send, size):
    got = [block]
    fwd = block
    bwd = block
    for _ in range((size - 1) // 2):
        fwd = send(fwd, 1)
        bwd = send(bwd, -1)
        got += [fwd, bwd]
    if size % 2 == 0:
        fwd = send(fwd, 1)
        got.append(fwd)
    return got


def replicate_gather(x, axes, count):
    copies = jnp.broadcast_to(x[None], (count,) + x.shape)
    got = lax.all_to_all(copies, axes, 0, 0, tiled=True)
    return got.reshape((count * x.shape[0],) + x.shape[1:])


DEV_AXES = ("y", "x", "c")


def shards(pool, nearest, center_owner, center_offset):
    owners = center_owner[0]
    offsets = center_offset[0]
    dev_count = lax.axis_size(DEV_AXES)
    z_count = lax.axis_size("z")
    x_count = lax.axis_size("x")
    y_count = lax.axis_size("y")
    my_index = lax.axis_index(DEV_AXES)
    per_device = owners.shape[0] // dev_count

    with jax.named_scope("compact_centers"):
        devices = jnp.arange(dev_count, dtype=jnp.int32)
        center_count = owners.shape[0]
        key = owners * center_count + jnp.arange(center_count, dtype=jnp.int32)
        position = jnp.sum((key[None, :] < key[:, None]).astype(jnp.int32), axis=1)
        to_peer = ((owners == my_index)[None, :]) & (
            (position % dev_count)[None, :] == devices[:, None]
        )
        peer_offset = jnp.sum(jnp.where(to_peer, offsets[None, :], 0), axis=1)
        send_rows = jnp.take(pool, peer_offset, axis=0)
        landed = lax.all_to_all(send_rows, DEV_AXES, 0, 0, tiled=True)
        wanted = my_index + dev_count * jnp.arange(per_device, dtype=jnp.int32)
        source = jnp.sum(
            jnp.where(position[None, :] == wanted[:, None], owners[None, :], 0), axis=1
        )
        compact = jnp.take(landed, source, axis=0)

    def y_send(x, s):
        return lax.ppermute(x, "y", [(i, (i + s) % y_count) for i in range(y_count)])

    row_norm = jnp.einsum("rd,rd->r", pool, pool, preferred_element_type=jnp.float32)

    def core_swap(x):
        return lax.ppermute(x, "c", [(0, 1), (1, 0)])

    def y_ring(block):
        near = y_send(block, 1), y_send(block, -1)
        split = block.shape[0] // 2
        far = y_send(near[0][:split], 1), y_send(near[1][split:], -1)
        return jnp.concatenate(near, axis=0), jnp.concatenate(far, axis=0)

    with jax.named_scope("spread_centers"):
        plane = replicate_gather(compact, ("z", "x"), z_count * x_count)
        split = plane.shape[0] // 2
        near_a, far_a = y_ring(plane[:split])
        near_b, far_b = y_ring(plane[split:])
        far = jnp.concatenate([far_a, far_b], axis=0)
        pieces = [plane, core_swap(plane), near_a, core_swap(near_a), near_b, core_swap(near_b)]
        pieces += [far, core_swap(far)]

    with jax.named_scope("distance_min"):
        running = nearest
        for piece in pieces:
            running = fold_chunk(pool, row_norm, running, piece)
    return running


def solution(mesh):
    grp_count = mesh.shape["grp"]
    dev_count = mesh.shape["dev"]
    y_count = dev_count // (X_CHIPS * CORES)
    torus = Mesh(mesh.devices.reshape(grp_count, y_count, X_CHIPS, CORES), ("z",) + DEV_AXES)
    rows = ("z",) + DEV_AXES
    in_specs = (P(rows, None), P(rows), P("z", None), P("z", None))
    out_specs = P(rows)
    return jax.shard_map(shards, mesh=torus, in_specs=in_specs, out_specs=out_specs, check_vma=False)
```

```python
import math

import jax
import jax.numpy as jnp
from jax import lax
from jax.experimental import pallas as pl
from jax.experimental.pallas import tpu as pltpu
from jax.sharding import Mesh, PartitionSpec as P

MOST = 32
X_CHIPS = 4
CORES = 2


def fold_chunk(pool_rows, row_norm, running, fragment):
    center_norm = jnp.einsum("cd,cd->c", fragment, fragment, preferred_element_type=jnp.float32)
    total_rows = pool_rows.shape[0]
    block = total_rows
    blocks = total_rows // block

    def one_block(args):
        block_rows, block_norm, block_near = args
        inner = lax.dot_general(
            block_rows, fragment, (((1,), (1,)), ((), ())), preferred_element_type=jnp.float32
        )
        distance = jnp.maximum(block_norm[:, None] + center_norm[None, :] - 2.0 * inner, 0.0)
        return jnp.minimum(block_near, jnp.min(distance, axis=1))

    result = lax.map(
        one_block,
        (
            pool_rows.reshape(blocks, block, pool_rows.shape[1]),
            row_norm.reshape(blocks, block),
            running.reshape(blocks, block),
        ),
    )
    return result.reshape(total_rows)


def ring_gather(block, send, size):
    got = [block]
    fwd = block
    bwd = block
    for _ in range((size - 1) // 2):
        fwd = send(fwd, 1)
        bwd = send(bwd, -1)
        got += [fwd, bwd]
    if size % 2 == 0:
        fwd = send(fwd, 1)
        got.append(fwd)
    return got


def _gather_rows_kernel(index_ref, table_ref, out_ref, sems):
    count = out_ref.shape[0]

    def copy(r):
        return pltpu.make_async_copy(
            table_ref.at[pl.ds(pl.multiple_of(index_ref[r] * 2, 2), 2)], out_ref.at[r], sems.at[r]
        )

    for r in range(count):
        copy(r).start()
    for r in range(count):
        copy(r).wait()


def gather_rows(table, index):
    count = index.shape[0]
    width = table.shape[1]
    index = jnp.clip(index // 2, 0, table.shape[0] // 2 - 1).astype(jnp.int32)
    return pl.pallas_call(
        _gather_rows_kernel,
        out_shape=jax.ShapeDtypeStruct((count, 2, width), table.dtype),
        in_specs=[pl.BlockSpec(memory_space=pltpu.SMEM), pl.BlockSpec(memory_space=pl.ANY)],
        out_specs=pl.BlockSpec(memory_space=pltpu.VMEM),
        scratch_shapes=[pltpu.SemaphoreType.DMA((count,))],
        cost_estimate=pl.CostEstimate(
            flops=0, bytes_accessed=2 * count * width * table.dtype.itemsize, transcendentals=0
        ),
    )(index, table)


def replicate_gather(x, axes, count):
    copies = jnp.broadcast_to(x[None], (count,) + x.shape)
    got = lax.all_to_all(copies, axes, 0, 0, tiled=True)
    return got.reshape((count * x.shape[0],) + x.shape[1:])


DEV_AXES = ("y", "x", "c")


def shards(pool, nearest, center_owner, center_offset):
    owners = center_owner[0]
    offsets = center_offset[0]
    dev_count = lax.axis_size(DEV_AXES)
    z_count = lax.axis_size("z")
    x_count = lax.axis_size("x")
    y_count = lax.axis_size("y")
    my_index = lax.axis_index(DEV_AXES)
    per_device = owners.shape[0] // dev_count

    with jax.named_scope("compact_centers"):
        devices = jnp.arange(dev_count, dtype=jnp.int32)
        center_count = owners.shape[0]
        key = owners * center_count + jnp.arange(center_count, dtype=jnp.int32)
        position = jnp.sum((key[None, :] < key[:, None]).astype(jnp.int32), axis=1)
        to_peer = ((owners == my_index)[None, :]) & (
            (position % dev_count)[None, :] == devices[:, None]
        )
        peer_offset = jnp.sum(jnp.where(to_peer, offsets[None, :], 0), axis=1)
        send_rows = gather_rows(pool, peer_offset)
        landed = lax.all_to_all(send_rows, DEV_AXES, 0, 0, tiled=True)
        wanted = my_index + dev_count * jnp.arange(per_device, dtype=jnp.int32)
        is_wanted = position[None, :] == wanted[:, None]
        source = jnp.sum(jnp.where(is_wanted, owners[None, :], 0), axis=1)
        parity = jnp.sum(jnp.where(is_wanted, offsets[None, :], 0), axis=1) % 2
        compact = jnp.take(landed.reshape(-1, landed.shape[-1]), source * 2 + parity, axis=0)

    def y_send(x, s):
        return lax.ppermute(x, "y", [(i, (i + s) % y_count) for i in range(y_count)])

    row_norm = jnp.einsum("rd,rd->r", pool, pool, preferred_element_type=jnp.float32)

    def core_swap(x):
        return lax.ppermute(x, "c", [(0, 1), (1, 0)])

    with jax.named_scope("spread_centers"):
        plane = replicate_gather(compact, ("z", "x"), z_count * x_count)
        y_near = y_send(plane, 1), y_send(plane, -1)
        split = plane.shape[0] // 2
        y_far = jnp.concatenate(
            [y_send(y_near[0][:split], 1), y_send(y_near[1][split:], -1)], axis=0
        )
        near = jnp.concatenate(y_near, axis=0)
        pieces = [plane, core_swap(plane), near, core_swap(near), y_far, core_swap(y_far)]

    with jax.named_scope("distance_min"):
        running = nearest
        for piece in pieces:
            running = fold_chunk(pool, row_norm, running, piece)
    return running


def solution(mesh):
    grp_count = mesh.shape["grp"]
    dev_count = mesh.shape["dev"]
    y_count = dev_count // (X_CHIPS * CORES)
    torus = Mesh(mesh.devices.reshape(grp_count, y_count, X_CHIPS, CORES), ("z",) + DEV_AXES)
    rows = ("z",) + DEV_AXES
    in_specs = (P(rows, None), P(rows), P("z", None), P("z", None))
    out_specs = P(rows)
    return jax.shard_map(shards, mesh=torus, in_specs=in_specs, out_specs=out_specs, check_vma=False)
```

```python
import math

import jax
import jax.numpy as jnp
from jax import lax
from jax.experimental import pallas as pl
from jax.experimental.pallas import tpu as pltpu
from jax.sharding import Mesh, PartitionSpec as P

MOST = 32
X_CHIPS = 4
CORES = 2


def fold_chunk(pool_rows, row_norm, running, fragment):
    center_norm = jnp.einsum("cd,cd->c", fragment, fragment, preferred_element_type=jnp.float32)
    total_rows = pool_rows.shape[0]
    block = total_rows
    blocks = total_rows // block

    def one_block(args):
        block_rows, block_norm, block_near = args
        inner = lax.dot_general(
            block_rows, fragment, (((1,), (1,)), ((), ())), preferred_element_type=jnp.float32
        )
        distance = jnp.maximum(block_norm[:, None] + center_norm[None, :] - 2.0 * inner, 0.0)
        return jnp.minimum(block_near, jnp.min(distance, axis=1))

    result = lax.map(
        one_block,
        (
            pool_rows.reshape(blocks, block, pool_rows.shape[1]),
            row_norm.reshape(blocks, block),
            running.reshape(blocks, block),
        ),
    )
    return result.reshape(total_rows)


def ring_gather(block, send, size):
    got = [block]
    fwd = block
    bwd = block
    for _ in range((size - 1) // 2):
        fwd = send(fwd, 1)
        bwd = send(bwd, -1)
        got += [fwd, bwd]
    if size % 2 == 0:
        fwd = send(fwd, 1)
        got.append(fwd)
    return got


def _gather_rows_kernel(index_ref, table_ref, out_ref, sems):
    count = out_ref.shape[0]

    def copy(r):
        return pltpu.make_async_copy(
            table_ref.at[pl.ds(pl.multiple_of(index_ref[r] * 2, 2), 2)], out_ref.at[r], sems.at[r]
        )

    for r in range(count):
        copy(r).start()
    for r in range(count):
        copy(r).wait()


def gather_rows(table, index):
    count = index.shape[0]
    width = table.shape[1]
    index = jnp.clip(index // 2, 0, table.shape[0] // 2 - 1).astype(jnp.int32)
    return pl.pallas_call(
        _gather_rows_kernel,
        out_shape=jax.ShapeDtypeStruct((count, 2, width), table.dtype),
        in_specs=[pl.BlockSpec(memory_space=pltpu.SMEM), pl.BlockSpec(memory_space=pl.ANY)],
        out_specs=pl.BlockSpec(memory_space=pltpu.VMEM),
        scratch_shapes=[pltpu.SemaphoreType.DMA((count,))],
        cost_estimate=pl.CostEstimate(
            flops=0, bytes_accessed=2 * count * width * table.dtype.itemsize, transcendentals=0
        ),
    )(index, table)


def replicate_gather(x, axes, count):
    copies = jnp.broadcast_to(x[None], (count,) + x.shape)
    got = lax.all_to_all(copies, axes, 0, 0, tiled=True)
    return got.reshape((count * x.shape[0],) + x.shape[1:])


DEV_AXES = ("y", "x", "c")


def shards(pool, nearest, center_owner, center_offset):
    owners = center_owner[0]
    offsets = center_offset[0]
    dev_count = lax.axis_size(DEV_AXES)
    z_count = lax.axis_size("z")
    x_count = lax.axis_size("x")
    y_count = lax.axis_size("y")
    my_index = lax.axis_index(DEV_AXES)
    per_device = owners.shape[0] // dev_count

    with jax.named_scope("compact_centers"):
        devices = jnp.arange(dev_count, dtype=jnp.int32)
        center_count = owners.shape[0]
        key = owners * center_count + jnp.arange(center_count, dtype=jnp.int32)
        position = jnp.sum((key[None, :] < key[:, None]).astype(jnp.int32), axis=1)
        to_peer = ((owners == my_index)[None, :]) & (
            (position % dev_count)[None, :] == devices[:, None]
        )
        peer_offset = jnp.sum(jnp.where(to_peer, offsets[None, :], 0), axis=1)
        send_rows = gather_rows(pool, peer_offset)
        landed = lax.all_to_all(send_rows, DEV_AXES, 0, 0, tiled=True)
        wanted = my_index + dev_count * jnp.arange(per_device, dtype=jnp.int32)
        is_wanted = position[None, :] == wanted[:, None]
        source = jnp.sum(jnp.where(is_wanted, owners[None, :], 0), axis=1)
        parity = jnp.sum(jnp.where(is_wanted, offsets[None, :], 0), axis=1) % 2
        compact = jnp.take(landed.reshape(-1, landed.shape[-1]), source * 2 + parity, axis=0)

    def y_send(x, s):
        return lax.ppermute(x, "y", [(i, (i + s) % y_count) for i in range(y_count)])

    row_norm = jnp.einsum("rd,rd->r", pool, pool, preferred_element_type=jnp.float32)

    def core_swap(x):
        return lax.ppermute(x, "c", [(0, 1), (1, 0)])

    with jax.named_scope("spread_centers"):
        plane = replicate_gather(compact, ("z", "x"), z_count * x_count)
        y_near = y_send(plane, 1), y_send(plane, -1)
        split = plane.shape[0] // 2
        y_far = jnp.concatenate(
            [y_send(y_near[0][:split], 1), y_send(y_near[1][split:], -1)], axis=0
        )
        near = jnp.concatenate(y_near, axis=0)
        both_planes = jnp.concatenate([plane, core_swap(plane)], axis=0)
        both_far = jnp.concatenate([y_far, core_swap(y_far)], axis=0)
        pieces = [both_planes, near, core_swap(near), both_far]

    with jax.named_scope("distance_min"):
        running = nearest
        for piece in pieces:
            running = fold_chunk(pool, row_norm, running, piece)
    return running


def solution(mesh):
    grp_count = mesh.shape["grp"]
    dev_count = mesh.shape["dev"]
    y_count = dev_count // (X_CHIPS * CORES)
    torus = Mesh(mesh.devices.reshape(grp_count, y_count, X_CHIPS, CORES), ("z",) + DEV_AXES)
    rows = ("z",) + DEV_AXES
    in_specs = (P(rows, None), P(rows), P("z", None), P("z", None))
    out_specs = P(rows)
    return jax.shard_map(shards, mesh=torus, in_specs=in_specs, out_specs=out_specs, check_vma=False)
```

```python
import math

import jax
import jax.numpy as jnp
from jax import lax
from jax.experimental import pallas as pl
from jax.experimental.pallas import tpu as pltpu
from jax.sharding import Mesh, PartitionSpec as P

MOST = 32
X_CHIPS = 4
CORES = 2


def fold_chunk(pool_rows, row_norm, running, fragment):
    center_norm = jnp.einsum("cd,cd->c", fragment, fragment, preferred_element_type=jnp.float32)
    total_rows = pool_rows.shape[0]
    block = total_rows
    blocks = total_rows // block

    def one_block(args):
        block_rows, block_norm, block_near = args
        inner = lax.dot_general(
            block_rows, fragment, (((1,), (1,)), ((), ())), preferred_element_type=jnp.float32
        )
        distance = jnp.maximum(block_norm[:, None] + center_norm[None, :] - 2.0 * inner, 0.0)
        return jnp.minimum(block_near, jnp.min(distance, axis=1))

    result = lax.map(
        one_block,
        (
            pool_rows.reshape(blocks, block, pool_rows.shape[1]),
            row_norm.reshape(blocks, block),
            running.reshape(blocks, block),
        ),
    )
    return result.reshape(total_rows)


def ring_gather(block, send, size):
    got = [block]
    fwd = block
    bwd = block
    for _ in range((size - 1) // 2):
        fwd = send(fwd, 1)
        bwd = send(bwd, -1)
        got += [fwd, bwd]
    if size % 2 == 0:
        fwd = send(fwd, 1)
        got.append(fwd)
    return got


def _gather_rows_kernel(index_ref, table_ref, out_ref, sems):
    count = out_ref.shape[0]

    def copy(r):
        return pltpu.make_async_copy(
            table_ref.at[pl.ds(pl.multiple_of(index_ref[r] * 2, 2), 2)], out_ref.at[r], sems.at[r]
        )

    for r in range(count):
        copy(r).start()
    for r in range(count):
        copy(r).wait()


def gather_rows(table, index):
    count = index.shape[0]
    width = table.shape[1]
    index = jnp.clip(index // 2, 0, table.shape[0] // 2 - 1).astype(jnp.int32)
    return pl.pallas_call(
        _gather_rows_kernel,
        out_shape=jax.ShapeDtypeStruct((count, 2, width), table.dtype),
        in_specs=[pl.BlockSpec(memory_space=pltpu.SMEM), pl.BlockSpec(memory_space=pl.ANY)],
        out_specs=pl.BlockSpec(memory_space=pltpu.VMEM),
        scratch_shapes=[pltpu.SemaphoreType.DMA((count,))],
        cost_estimate=pl.CostEstimate(
            flops=0, bytes_accessed=2 * count * width * table.dtype.itemsize, transcendentals=0
        ),
    )(index, table)


def replicate_gather(x, axes, count):
    copies = jnp.broadcast_to(x[None], (count,) + x.shape)
    got = lax.all_to_all(copies, axes, 0, 0, tiled=True)
    return got.reshape((count * x.shape[0],) + x.shape[1:])


DEV_AXES = ("y", "x", "c")


def shards(pool, nearest, center_owner, center_offset):
    owners = center_owner[0]
    offsets = center_offset[0]
    dev_count = lax.axis_size(DEV_AXES)
    z_count = lax.axis_size("z")
    x_count = lax.axis_size("x")
    y_count = lax.axis_size("y")
    my_index = lax.axis_index(DEV_AXES)
    devices = jnp.arange(dev_count, dtype=jnp.int32)

    with jax.named_scope("compact_centers"):
        columns = y_count * lax.axis_size("c")
        slots = -(-MOST // columns)
        center_count = owners.shape[0]
        key = owners * center_count + jnp.arange(center_count, dtype=jnp.int32)
        position = jnp.sum((key[None, :] < key[:, None]).astype(jnp.int32), axis=1)
        owner_start = jnp.sum((owners[None, :] < owners[:, None]).astype(jnp.int32), axis=1)
        rank = position - owner_start
        mine_mask = owners == my_index
        my_start = jnp.sum((owners < my_index).astype(jnp.int32))
        ranks = jnp.arange(MOST, dtype=jnp.int32)
        rank_offset = jnp.sum(
            jnp.where(mine_mask[None, :] & (rank[None, :] == ranks[:, None]), offsets[None, :], 0),
            axis=1,
        )
        pairs = gather_rows(pool, rank_offset)
        peer_column = (devices // (x_count * 2)) * 2 + devices % 2
        send_rank = ((peer_column[:, None] - my_start) % columns) + columns * jnp.arange(
            slots, dtype=jnp.int32
        )[None, :]
        send_rank = jnp.minimum(send_rank, MOST - 1).reshape(-1)
        send_parity = jnp.sum(
            jnp.where(send_rank[:, None] == ranks[None, :], rank_offset[None, :] % 2, 0), axis=1
        )
        send_rows = jnp.take(pairs.reshape(-1, pairs.shape[-1]), send_rank * 2 + send_parity, axis=0)
        send_rows = send_rows.reshape(dev_count, slots, send_rows.shape[-1])
        landed = lax.all_to_all(send_rows, DEV_AXES, 0, 0, tiled=True)
        my_column = lax.axis_index("y") * 2 + lax.axis_index("c")
        wanted = my_column + columns * jnp.arange(center_count // columns, dtype=jnp.int32)
        is_wanted = position[None, :] == wanted[:, None]
        source = jnp.sum(jnp.where(is_wanted, owners[None, :], 0), axis=1)
        source_start = jnp.sum(jnp.where(is_wanted, owner_start[None, :], 0), axis=1)
        slot = (wanted - source_start) // columns
        column_rows = jnp.take(
            landed.reshape(-1, landed.shape[-1]), source * slots + slot, axis=0
        )

    def y_send(x, s):
        return lax.ppermute(x, "y", [(i, (i + s) % y_count) for i in range(y_count)])

    row_norm = jnp.einsum("rd,rd->r", pool, pool, preferred_element_type=jnp.float32)

    def core_swap(x):
        return lax.ppermute(x, "c", [(0, 1), (1, 0)])

    with jax.named_scope("spread_centers"):
        plane = replicate_gather(column_rows, "z", z_count)
        y_near = y_send(plane, 1), y_send(plane, -1)
        split = plane.shape[0] // 2
        y_far = jnp.concatenate(
            [y_send(y_near[0][:split], 1), y_send(y_near[1][split:], -1)], axis=0
        )
        near = jnp.concatenate(y_near, axis=0)
        pieces = [plane, core_swap(plane), near, core_swap(near), y_far, core_swap(y_far)]

    with jax.named_scope("distance_min"):
        running = nearest
        for piece in pieces:
            running = fold_chunk(pool, row_norm, running, piece)
    return running


def solution(mesh):
    grp_count = mesh.shape["grp"]
    dev_count = mesh.shape["dev"]
    y_count = dev_count // (X_CHIPS * CORES)
    torus = Mesh(mesh.devices.reshape(grp_count, y_count, X_CHIPS, CORES), ("z",) + DEV_AXES)
    rows = ("z",) + DEV_AXES
    in_specs = (P(rows, None), P(rows), P("z", None), P("z", None))
    out_specs = P(rows)
    return jax.shard_map(shards, mesh=torus, in_specs=in_specs, out_specs=out_specs, check_vma=False)
```

```python
import math

import jax
import jax.numpy as jnp
from jax import lax
from jax.experimental import pallas as pl
from jax.experimental.pallas import tpu as pltpu
from jax.sharding import Mesh, PartitionSpec as P

MOST = 32
X_CHIPS = 4
CORES = 2


def fold_chunk(pool_rows, row_norm, running, fragment):
    center_norm = jnp.einsum("cd,cd->c", fragment, fragment, preferred_element_type=jnp.float32)
    total_rows = pool_rows.shape[0]
    block = total_rows
    blocks = total_rows // block

    def one_block(args):
        block_rows, block_norm, block_near = args
        inner = lax.dot_general(
            block_rows, fragment, (((1,), (1,)), ((), ())), preferred_element_type=jnp.float32
        )
        distance = jnp.maximum(block_norm[:, None] + center_norm[None, :] - 2.0 * inner, 0.0)
        return jnp.min(jnp.minimum(distance, block_near[:, None]), axis=1)

    result = lax.map(
        one_block,
        (
            pool_rows.reshape(blocks, block, pool_rows.shape[1]),
            row_norm.reshape(blocks, block),
            running.reshape(blocks, block),
        ),
    )
    return result.reshape(total_rows)


def ring_gather(block, send, size):
    got = [block]
    fwd = block
    bwd = block
    for _ in range((size - 1) // 2):
        fwd = send(fwd, 1)
        bwd = send(bwd, -1)
        got += [fwd, bwd]
    if size % 2 == 0:
        fwd = send(fwd, 1)
        got.append(fwd)
    return got


def _gather_rows_kernel(index_ref, table_ref, out_ref, sems):
    count = out_ref.shape[0]

    def copy(r):
        return pltpu.make_async_copy(
            table_ref.at[pl.ds(pl.multiple_of(index_ref[r] * 2, 2), 2)], out_ref.at[r], sems.at[r]
        )

    for r in range(count):
        copy(r).start()
    for r in range(count):
        copy(r).wait()


def gather_rows(table, index):
    count = index.shape[0]
    width = table.shape[1]
    index = jnp.clip(index // 2, 0, table.shape[0] // 2 - 1).astype(jnp.int32)
    return pl.pallas_call(
        _gather_rows_kernel,
        out_shape=jax.ShapeDtypeStruct((count, 2, width), table.dtype),
        in_specs=[pl.BlockSpec(memory_space=pltpu.SMEM), pl.BlockSpec(memory_space=pl.ANY)],
        out_specs=pl.BlockSpec(memory_space=pltpu.VMEM),
        scratch_shapes=[pltpu.SemaphoreType.DMA((count,))],
        cost_estimate=pl.CostEstimate(
            flops=0, bytes_accessed=2 * count * width * table.dtype.itemsize, transcendentals=0
        ),
    )(index, table)


def replicate_gather(x, axes, count):
    copies = jnp.broadcast_to(x[None], (count,) + x.shape)
    got = lax.all_to_all(copies, axes, 0, 0, tiled=True)
    return got.reshape((count * x.shape[0],) + x.shape[1:])


DEV_AXES = ("y", "x", "c")


def shards(pool, nearest, center_owner, center_offset):
    owners = center_owner[0]
    offsets = center_offset[0]
    dev_count = lax.axis_size(DEV_AXES)
    z_count = lax.axis_size("z")
    x_count = lax.axis_size("x")
    y_count = lax.axis_size("y")
    my_index = lax.axis_index(DEV_AXES)
    per_device = owners.shape[0] // dev_count

    with jax.named_scope("compact_centers"):
        devices = jnp.arange(dev_count, dtype=jnp.int32)
        center_count = owners.shape[0]
        key = owners * center_count + jnp.arange(center_count, dtype=jnp.int32)
        position = jnp.sum((key[None, :] < key[:, None]).astype(jnp.int32), axis=1)
        to_peer = ((owners == my_index)[None, :]) & (
            (position % dev_count)[None, :] == devices[:, None]
        )
        peer_offset = jnp.sum(jnp.where(to_peer, offsets[None, :], 0), axis=1)
        send_rows = gather_rows(pool, peer_offset)
        landed = lax.all_to_all(send_rows, DEV_AXES, 0, 0, tiled=True)
        wanted = my_index + dev_count * jnp.arange(per_device, dtype=jnp.int32)
        is_wanted = position[None, :] == wanted[:, None]
        source = jnp.sum(jnp.where(is_wanted, owners[None, :], 0), axis=1)
        parity = jnp.sum(jnp.where(is_wanted, offsets[None, :], 0), axis=1) % 2
        compact = jnp.take(landed.reshape(-1, landed.shape[-1]), source * 2 + parity, axis=0)

    def y_send(x, s):
        return lax.ppermute(x, "y", [(i, (i + s) % y_count) for i in range(y_count)])

    row_norm = jnp.einsum("rd,rd->r", pool, pool, preferred_element_type=jnp.float32)

    def core_swap(x):
        return lax.ppermute(x, "c", [(0, 1), (1, 0)])

    with jax.named_scope("spread_centers"):
        plane = replicate_gather(compact, ("z", "x"), z_count * x_count)
        y_near = y_send(plane, 1), y_send(plane, -1)
        split = plane.shape[0] // 2
        y_far = jnp.concatenate(
            [y_send(y_near[0][:split], 1), y_send(y_near[1][split:], -1)], axis=0
        )
        near = jnp.concatenate(y_near, axis=0)
        pieces = [plane, core_swap(plane), near, core_swap(near), y_far, core_swap(y_far)]

    with jax.named_scope("distance_min"):
        running = nearest
        for piece in pieces:
            running = fold_chunk(pool, row_norm, running, piece)
    return running


def solution(mesh):
    grp_count = mesh.shape["grp"]
    dev_count = mesh.shape["dev"]
    y_count = dev_count // (X_CHIPS * CORES)
    torus = Mesh(mesh.devices.reshape(grp_count, y_count, X_CHIPS, CORES), ("z",) + DEV_AXES)
    rows = ("z",) + DEV_AXES
    in_specs = (P(rows, None), P(rows), P("z", None), P("z", None))
    out_specs = P(rows)
    return jax.shard_map(shards, mesh=torus, in_specs=in_specs, out_specs=out_specs, check_vma=False)
```

```python
import math

import jax
import jax.numpy as jnp
from jax import lax
from jax.experimental import pallas as pl
from jax.experimental.pallas import tpu as pltpu
from jax.sharding import Mesh, PartitionSpec as P

MOST = 32
X_CHIPS = 4
CORES = 2


def fold_chunk(pool_rows, row_norm, running, fragment):
    center_norm = jnp.einsum("cd,cd->c", fragment, fragment, preferred_element_type=jnp.float32)
    total_rows = pool_rows.shape[0]
    block = total_rows
    blocks = total_rows // block

    def one_block(args):
        block_rows, block_norm, block_near = args
        inner = lax.dot_general(
            block_rows, fragment, (((1,), (1,)), ((), ())), preferred_element_type=jnp.float32
        )
        distance = jnp.maximum(block_norm[:, None] + center_norm[None, :] - 2.0 * inner, 0.0)
        return jnp.minimum(block_near, jnp.min(distance, axis=1))

    result = lax.map(
        one_block,
        (
            pool_rows.reshape(blocks, block, pool_rows.shape[1]),
            row_norm.reshape(blocks, block),
            running.reshape(blocks, block),
        ),
    )
    return result.reshape(total_rows)


def ring_gather(block, send, size):
    got = [block]
    fwd = block
    bwd = block
    for _ in range((size - 1) // 2):
        fwd = send(fwd, 1)
        bwd = send(bwd, -1)
        got += [fwd, bwd]
    if size % 2 == 0:
        fwd = send(fwd, 1)
        got.append(fwd)
    return got


def _gather_rows_kernel(index_ref, table_ref, out_ref, sems):
    count = out_ref.shape[0]

    def copy(r):
        return pltpu.make_async_copy(
            table_ref.at[pl.ds(pl.multiple_of(index_ref[r] * 2, 2), 2)], out_ref.at[r], sems.at[r]
        )

    for r in range(count):
        copy(r).start()
    for r in range(count):
        copy(r).wait()


def gather_rows(table, index):
    count = index.shape[0]
    width = table.shape[1]
    index = jnp.clip(index // 2, 0, table.shape[0] // 2 - 1).astype(jnp.int32)
    return pl.pallas_call(
        _gather_rows_kernel,
        out_shape=jax.ShapeDtypeStruct((count, 2, width), table.dtype),
        in_specs=[pl.BlockSpec(memory_space=pltpu.SMEM), pl.BlockSpec(memory_space=pl.ANY)],
        out_specs=pl.BlockSpec(memory_space=pltpu.VMEM),
        scratch_shapes=[pltpu.SemaphoreType.DMA((count,))],
        cost_estimate=pl.CostEstimate(
            flops=0, bytes_accessed=2 * count * width * table.dtype.itemsize, transcendentals=0
        ),
    )(index, table)


def replicate_gather(x, axes, count):
    copies = jnp.broadcast_to(x[None], (count,) + x.shape)
    got = lax.all_to_all(copies, axes, 0, 0, tiled=True)
    return got.reshape((count * x.shape[0],) + x.shape[1:])


DEV_AXES = ("y", "x", "c")


def shards(pool, nearest, center_owner, center_offset):
    owners = center_owner[0]
    offsets = center_offset[0]
    dev_count = lax.axis_size(DEV_AXES)
    z_count = lax.axis_size("z")
    x_count = lax.axis_size("x")
    y_count = lax.axis_size("y")
    my_index = lax.axis_index(DEV_AXES)
    per_device = owners.shape[0] // dev_count

    with jax.named_scope("compact_centers"):
        devices = jnp.arange(dev_count, dtype=jnp.int32)
        center_count = owners.shape[0]
        order = lax.broadcasted_iota(jnp.int32, (center_count, center_count), 1) < lax.broadcasted_iota(
            jnp.int32, (center_count, center_count), 0
        )
        before = (owners[None, :] < owners[:, None]) | (
            (owners[None, :] == owners[:, None]) & order
        )
        position = jnp.sum(before.astype(jnp.int32), axis=1)
        to_peer = ((owners == my_index)[None, :]) & (
            (position % dev_count)[None, :] == devices[:, None]
        )
        peer_offset = jnp.sum(jnp.where(to_peer, offsets[None, :], 0), axis=1)
        send_rows = gather_rows(pool, peer_offset)
        landed = lax.all_to_all(send_rows, DEV_AXES, 0, 0, tiled=True)
        wanted = my_index + dev_count * jnp.arange(per_device, dtype=jnp.int32)
        is_wanted = position[None, :] == wanted[:, None]
        source = jnp.sum(jnp.where(is_wanted, owners[None, :], 0), axis=1)
        parity = jnp.sum(jnp.where(is_wanted, offsets[None, :], 0), axis=1) % 2
        compact = jnp.take(landed.reshape(-1, landed.shape[-1]), source * 2 + parity, axis=0)

    def y_send(x, s):
        return lax.ppermute(x, "y", [(i, (i + s) % y_count) for i in range(y_count)])

    row_norm = jnp.einsum("rd,rd->r", pool, pool, preferred_element_type=jnp.float32)

    def core_swap(x):
        return lax.ppermute(x, "c", [(0, 1), (1, 0)])

    with jax.named_scope("spread_centers"):
        plane = replicate_gather(compact, ("z", "x"), z_count * x_count)
        y_near = y_send(plane, 1), y_send(plane, -1)
        split = plane.shape[0] // 2
        y_far = jnp.concatenate(
            [y_send(y_near[0][:split], 1), y_send(y_near[1][split:], -1)], axis=0
        )
        near = jnp.concatenate(y_near, axis=0)
        pieces = [plane, core_swap(plane), near, core_swap(near), y_far, core_swap(y_far)]

    with jax.named_scope("distance_min"):
        running = nearest
        for piece in pieces:
            running = fold_chunk(pool, row_norm, running, piece)
    return running


def solution(mesh):
    grp_count = mesh.shape["grp"]
    dev_count = mesh.shape["dev"]
    y_count = dev_count // (X_CHIPS * CORES)
    torus = Mesh(mesh.devices.reshape(grp_count, y_count, X_CHIPS, CORES), ("z",) + DEV_AXES)
    rows = ("z",) + DEV_AXES
    in_specs = (P(rows, None), P(rows), P("z", None), P("z", None))
    out_specs = P(rows)
    return jax.shard_map(shards, mesh=torus, in_specs=in_specs, out_specs=out_specs, check_vma=False)
```

```python
import math

import jax
import jax.numpy as jnp
from jax import lax
from jax.experimental import pallas as pl
from jax.experimental.pallas import tpu as pltpu
from jax.sharding import Mesh, PartitionSpec as P

MOST = 32
X_CHIPS = 4
CORES = 2


def _fold_kernel(frag_ref, center_norm_ref, rows_ref, row_norm_ref, running_ref, out_ref):
    inner = lax.dot_general(
        frag_ref[...], rows_ref[...], (((1,), (1,)), ((), ())), preferred_element_type=jnp.float32
    )
    distance = jnp.maximum(row_norm_ref[...] + center_norm_ref[...] - 2.0 * inner, 0.0)
    out_ref[...] = jnp.minimum(running_ref[...], jnp.min(distance, axis=0, keepdims=True))


def fold_chunk(pool_rows, row_norm, running, fragment):
    center_norm = jnp.einsum("cd,cd->c", fragment, fragment, preferred_element_type=jnp.float32)
    total_rows, width = pool_rows.shape
    count = fragment.shape[0]
    block = math.gcd(total_rows, 1024)
    result = pl.pallas_call(
        _fold_kernel,
        out_shape=jax.ShapeDtypeStruct((1, total_rows), jnp.float32),
        grid=(total_rows // block,),
        in_specs=[
            pl.BlockSpec((count, width), lambda i: (0, 0)),
            pl.BlockSpec((count, 1), lambda i: (0, 0)),
            pl.BlockSpec((block, width), lambda i: (i, 0)),
            pl.BlockSpec((1, block), lambda i: (0, i)),
            pl.BlockSpec((1, block), lambda i: (0, i)),
        ],
        out_specs=pl.BlockSpec((1, block), lambda i: (0, i)),
        cost_estimate=pl.CostEstimate(
            flops=2 * count * total_rows * width,
            bytes_accessed=2 * (total_rows + count) * width + 12 * total_rows,
            transcendentals=0,
        ),
    )(
        fragment,
        center_norm.reshape(count, 1),
        pool_rows,
        row_norm.reshape(1, total_rows),
        running.reshape(1, total_rows),
    )
    return result.reshape(total_rows)


def ring_gather(block, send, size):
    got = [block]
    fwd = block
    bwd = block
    for _ in range((size - 1) // 2):
        fwd = send(fwd, 1)
        bwd = send(bwd, -1)
        got += [fwd, bwd]
    if size % 2 == 0:
        fwd = send(fwd, 1)
        got.append(fwd)
    return got


def _gather_rows_kernel(index_ref, table_ref, out_ref, sems):
    count = out_ref.shape[0]

    def copy(r):
        return pltpu.make_async_copy(
            table_ref.at[pl.ds(pl.multiple_of(index_ref[r] * 2, 2), 2)], out_ref.at[r], sems.at[r]
        )

    for r in range(count):
        copy(r).start()
    for r in range(count):
        copy(r).wait()


def gather_rows(table, index):
    count = index.shape[0]
    width = table.shape[1]
    index = jnp.clip(index // 2, 0, table.shape[0] // 2 - 1).astype(jnp.int32)
    return pl.pallas_call(
        _gather_rows_kernel,
        out_shape=jax.ShapeDtypeStruct((count, 2, width), table.dtype),
        in_specs=[pl.BlockSpec(memory_space=pltpu.SMEM), pl.BlockSpec(memory_space=pl.ANY)],
        out_specs=pl.BlockSpec(memory_space=pltpu.VMEM),
        scratch_shapes=[pltpu.SemaphoreType.DMA((count,))],
        cost_estimate=pl.CostEstimate(
            flops=0, bytes_accessed=2 * count * width * table.dtype.itemsize, transcendentals=0
        ),
    )(index, table)


def replicate_gather(x, axes, count):
    copies = jnp.broadcast_to(x[None], (count,) + x.shape)
    got = lax.all_to_all(copies, axes, 0, 0, tiled=True)
    return got.reshape((count * x.shape[0],) + x.shape[1:])


DEV_AXES = ("y", "x", "c")


def shards(pool, nearest, center_owner, center_offset):
    owners = center_owner[0]
    offsets = center_offset[0]
    dev_count = lax.axis_size(DEV_AXES)
    z_count = lax.axis_size("z")
    x_count = lax.axis_size("x")
    y_count = lax.axis_size("y")
    my_index = lax.axis_index(DEV_AXES)
    per_device = owners.shape[0] // dev_count

    with jax.named_scope("compact_centers"):
        devices = jnp.arange(dev_count, dtype=jnp.int32)
        center_count = owners.shape[0]
        order = lax.broadcasted_iota(jnp.int32, (center_count, center_count), 1) < lax.broadcasted_iota(
            jnp.int32, (center_count, center_count), 0
        )
        before = (owners[None, :] < owners[:, None]) | (
            (owners[None, :] == owners[:, None]) & order
        )
        position = jnp.sum(before.astype(jnp.int32), axis=1)
        to_peer = ((owners == my_index)[None, :]) & (
            (position % dev_count)[None, :] == devices[:, None]
        )
        peer_offset = jnp.sum(jnp.where(to_peer, offsets[None, :], 0), axis=1)
        send_rows = gather_rows(pool, peer_offset)
        landed = lax.all_to_all(send_rows, DEV_AXES, 0, 0, tiled=True)
        wanted = my_index + dev_count * jnp.arange(per_device, dtype=jnp.int32)
        is_wanted = position[None, :] == wanted[:, None]
        source = jnp.sum(jnp.where(is_wanted, owners[None, :], 0), axis=1)
        parity = jnp.sum(jnp.where(is_wanted, offsets[None, :], 0), axis=1) % 2
        compact = jnp.take(landed.reshape(-1, landed.shape[-1]), source * 2 + parity, axis=0)

    def y_send(x, s):
        return lax.ppermute(x, "y", [(i, (i + s) % y_count) for i in range(y_count)])

    row_norm = jnp.einsum("rd,rd->r", pool, pool, preferred_element_type=jnp.float32)

    def core_swap(x):
        return lax.ppermute(x, "c", [(0, 1), (1, 0)])

    with jax.named_scope("spread_centers"):
        plane = replicate_gather(compact, ("z", "x"), z_count * x_count)
        y_near = y_send(plane, 1), y_send(plane, -1)
        split = plane.shape[0] // 2
        y_far = jnp.concatenate(
            [y_send(y_near[0][:split], 1), y_send(y_near[1][split:], -1)], axis=0
        )
        near = jnp.concatenate(y_near, axis=0)
        pieces = [plane, core_swap(plane), near, core_swap(near), y_far, core_swap(y_far)]

    with jax.named_scope("distance_min"):
        running = nearest
        for piece in pieces:
            running = fold_chunk(pool, row_norm, running, piece)
    return running


def solution(mesh):
    grp_count = mesh.shape["grp"]
    dev_count = mesh.shape["dev"]
    y_count = dev_count // (X_CHIPS * CORES)
    torus = Mesh(mesh.devices.reshape(grp_count, y_count, X_CHIPS, CORES), ("z",) + DEV_AXES)
    rows = ("z",) + DEV_AXES
    in_specs = (P(rows, None), P(rows), P("z", None), P("z", None))
    out_specs = P(rows)
    return jax.shard_map(shards, mesh=torus, in_specs=in_specs, out_specs=out_specs, check_vma=False)
```

```python
import math

import jax
import jax.numpy as jnp
from jax import lax
from jax.experimental import pallas as pl
from jax.experimental.pallas import tpu as pltpu
from jax.sharding import Mesh, PartitionSpec as P

MOST = 32
X_CHIPS = 4
CORES = 2


def fold_chunk(pool_rows, row_norm, running, fragment):
    center_norm = jnp.einsum("cd,cd->c", fragment, fragment, preferred_element_type=jnp.float32)
    total_rows = pool_rows.shape[0]
    block = total_rows
    blocks = total_rows // block

    def one_block(args):
        block_rows, block_norm, block_near = args
        inner = lax.dot_general(
            block_rows, fragment, (((1,), (1,)), ((), ())), preferred_element_type=jnp.float32
        )
        distance = jnp.maximum(block_norm[:, None] + center_norm[None, :] - 2.0 * inner, 0.0)
        return jnp.minimum(block_near, jnp.min(distance, axis=1))

    result = lax.map(
        one_block,
        (
            pool_rows.reshape(blocks, block, pool_rows.shape[1]),
            row_norm.reshape(blocks, block),
            running.reshape(blocks, block),
        ),
    )
    return result.reshape(total_rows)


def ring_gather(block, send, size):
    got = [block]
    fwd = block
    bwd = block
    for _ in range((size - 1) // 2):
        fwd = send(fwd, 1)
        bwd = send(bwd, -1)
        got += [fwd, bwd]
    if size % 2 == 0:
        fwd = send(fwd, 1)
        got.append(fwd)
    return got


def _gather_rows_kernel(index_ref, table_ref, out_ref, sems):
    count = out_ref.shape[0]

    def copy(r):
        return pltpu.make_async_copy(
            table_ref.at[pl.ds(pl.multiple_of(index_ref[r] * 2, 2), 2)], out_ref.at[r], sems.at[r]
        )

    for r in range(count):
        copy(r).start()
    for r in range(count):
        copy(r).wait()


def gather_rows(table, index):
    count = index.shape[0]
    width = table.shape[1]
    index = jnp.clip(index // 2, 0, table.shape[0] // 2 - 1).astype(jnp.int32)
    return pl.pallas_call(
        _gather_rows_kernel,
        out_shape=jax.ShapeDtypeStruct((count, 2, width), table.dtype),
        in_specs=[pl.BlockSpec(memory_space=pltpu.SMEM), pl.BlockSpec(memory_space=pl.ANY)],
        out_specs=pl.BlockSpec(memory_space=pltpu.VMEM),
        scratch_shapes=[pltpu.SemaphoreType.DMA((count,))],
        cost_estimate=pl.CostEstimate(
            flops=0, bytes_accessed=2 * count * width * table.dtype.itemsize, transcendentals=0
        ),
    )(index, table)


def replicate_gather(x, axes, count):
    copies = jnp.broadcast_to(x[None], (count,) + x.shape)
    got = lax.all_to_all(copies, axes, 0, 0, tiled=True)
    return got.reshape((count * x.shape[0],) + x.shape[1:])


DEV_AXES = ("y", "x", "c")


def shards(pool, nearest, center_owner, center_offset):
    owners = center_owner[0]
    offsets = center_offset[0]
    dev_count = lax.axis_size(DEV_AXES)
    z_count = lax.axis_size("z")
    x_count = lax.axis_size("x")
    y_count = lax.axis_size("y")
    my_index = lax.axis_index(DEV_AXES)
    per_device = owners.shape[0] // dev_count

    with jax.named_scope("compact_centers"):
        devices = jnp.arange(dev_count, dtype=jnp.int32)
        center_count = owners.shape[0]
        order = lax.broadcasted_iota(jnp.int32, (center_count, center_count), 1) < lax.broadcasted_iota(
            jnp.int32, (center_count, center_count), 0
        )
        before = (owners[None, :] < owners[:, None]) | (
            (owners[None, :] == owners[:, None]) & order
        )
        position = jnp.sum(before.astype(jnp.int32), axis=1)
        to_peer = ((owners == my_index)[None, :]) & (
            (position % dev_count)[None, :] == devices[:, None]
        )
        peer_offset = jnp.sum(jnp.where(to_peer, offsets[None, :], 0), axis=1)
        send_rows = gather_rows(pool, peer_offset)
        landed = lax.all_to_all(send_rows, DEV_AXES, 0, 0, tiled=True)
        wanted = my_index + dev_count * jnp.arange(per_device, dtype=jnp.int32)
        is_wanted = position[None, :] == wanted[:, None]
        source = jnp.sum(jnp.where(is_wanted, owners[None, :], 0), axis=1)
        parity = jnp.sum(jnp.where(is_wanted, offsets[None, :], 0), axis=1) % 2
        compact = jnp.take(landed.reshape(-1, landed.shape[-1]), source * 2 + parity, axis=0)

    def y_send(x, s):
        return lax.ppermute(x, "y", [(i, (i + s) % y_count) for i in range(y_count)])

    row_norm = jnp.einsum("rd,rd->r", pool, pool, preferred_element_type=jnp.float32)

    def core_swap(x):
        return lax.ppermute(x, "c", [(0, 1), (1, 0)])

    with jax.named_scope("spread_centers"):
        plane = replicate_gather(compact, ("z", "x"), z_count * x_count)
        y_near = y_send(plane, 1), y_send(plane, -1)
        split = plane.shape[0] // 2
        y_far = jnp.concatenate(
            [y_send(y_near[0][:split], 1), y_send(y_near[1][split:], -1)], axis=0
        )
        near = jnp.concatenate(y_near, axis=0)
        both_near = jnp.concatenate([near, core_swap(near)], axis=0)
        both_far = jnp.concatenate([y_far, core_swap(y_far)], axis=0)
        pieces = [plane, core_swap(plane), both_near, both_far]

    with jax.named_scope("distance_min"):
        running = nearest
        for piece in pieces:
            running = fold_chunk(pool, row_norm, running, piece)
    return running


def solution(mesh):
    grp_count = mesh.shape["grp"]
    dev_count = mesh.shape["dev"]
    y_count = dev_count // (X_CHIPS * CORES)
    torus = Mesh(mesh.devices.reshape(grp_count, y_count, X_CHIPS, CORES), ("z",) + DEV_AXES)
    rows = ("z",) + DEV_AXES
    in_specs = (P(rows, None), P(rows), P("z", None), P("z", None))
    out_specs = P(rows)
    return jax.shard_map(shards, mesh=torus, in_specs=in_specs, out_specs=out_specs, check_vma=False)
```

```python
import math

import jax
import jax.numpy as jnp
from jax import lax
from jax.experimental import pallas as pl
from jax.experimental.pallas import tpu as pltpu
from jax.sharding import Mesh, PartitionSpec as P

MOST = 32
X_CHIPS = 4
CORES = 2


def fold_chunk(pool_rows, row_norm, running, fragment):
    center_norm = jnp.einsum("cd,cd->c", fragment, fragment, preferred_element_type=jnp.float32)
    total_rows = pool_rows.shape[0]
    block = total_rows
    blocks = total_rows // block

    def one_block(args):
        block_rows, block_norm, block_near = args
        inner = lax.dot_general(
            block_rows, fragment, (((1,), (1,)), ((), ())), preferred_element_type=jnp.float32
        )
        distance = jnp.maximum(block_norm[:, None] + center_norm[None, :] - 2.0 * inner, 0.0)
        return jnp.minimum(block_near, jnp.min(distance, axis=1))

    result = lax.map(
        one_block,
        (
            pool_rows.reshape(blocks, block, pool_rows.shape[1]),
            row_norm.reshape(blocks, block),
            running.reshape(blocks, block),
        ),
    )
    return result.reshape(total_rows)


def ring_gather(block, send, size):
    got = [block]
    fwd = block
    bwd = block
    for _ in range((size - 1) // 2):
        fwd = send(fwd, 1)
        bwd = send(bwd, -1)
        got += [fwd, bwd]
    if size % 2 == 0:
        fwd = send(fwd, 1)
        got.append(fwd)
    return got


def _gather_rows_kernel(index_ref, table_ref, out_ref, sems):
    count = out_ref.shape[0]

    def copy(r):
        return pltpu.make_async_copy(
            table_ref.at[pl.ds(pl.multiple_of(index_ref[r] * 2, 2), 2)], out_ref.at[r], sems.at[r]
        )

    for r in range(count):
        copy(r).start()
    for r in range(count):
        copy(r).wait()


def gather_rows(table, index):
    count = index.shape[0]
    width = table.shape[1]
    index = jnp.clip(index // 2, 0, table.shape[0] // 2 - 1).astype(jnp.int32)
    return pl.pallas_call(
        _gather_rows_kernel,
        out_shape=jax.ShapeDtypeStruct((count, 2, width), table.dtype),
        in_specs=[pl.BlockSpec(memory_space=pltpu.SMEM), pl.BlockSpec(memory_space=pl.ANY)],
        out_specs=pl.BlockSpec(memory_space=pltpu.VMEM),
        scratch_shapes=[pltpu.SemaphoreType.DMA((count,))],
        cost_estimate=pl.CostEstimate(
            flops=0, bytes_accessed=2 * count * width * table.dtype.itemsize, transcendentals=0
        ),
    )(index, table)


def replicate_gather(x, axes, count):
    copies = jnp.broadcast_to(x[None], (count,) + x.shape)
    got = lax.all_to_all(copies, axes, 0, 0, tiled=True)
    return got.reshape((count * x.shape[0],) + x.shape[1:])


DEV_AXES = ("y", "x", "c")


def shards(pool, nearest, center_owner, center_offset):
    owners = center_owner[0]
    offsets = center_offset[0]
    dev_count = lax.axis_size(DEV_AXES)
    z_count = lax.axis_size("z")
    x_count = lax.axis_size("x")
    y_count = lax.axis_size("y")
    my_index = lax.axis_index(DEV_AXES)
    per_device = owners.shape[0] // dev_count

    with jax.named_scope("compact_centers"):
        devices = jnp.arange(dev_count, dtype=jnp.int32)
        center_count = owners.shape[0]
        order = lax.broadcasted_iota(jnp.int32, (center_count, center_count), 1) < lax.broadcasted_iota(
            jnp.int32, (center_count, center_count), 0
        )
        before = (owners[None, :] < owners[:, None]) | (
            (owners[None, :] == owners[:, None]) & order
        )
        position = jnp.sum(before.astype(jnp.int32), axis=1)
        to_peer = ((owners == my_index)[None, :]) & (
            (position % dev_count)[None, :] == devices[:, None]
        )
        peer_offset = jnp.sum(jnp.where(to_peer, offsets[None, :], 0), axis=1)
        send_rows = gather_rows(pool, peer_offset)
        landed = lax.all_to_all(send_rows, DEV_AXES, 0, 0, tiled=True)
        wanted = my_index + dev_count * jnp.arange(per_device, dtype=jnp.int32)
        is_wanted = position[None, :] == wanted[:, None]
        source = jnp.sum(jnp.where(is_wanted, owners[None, :], 0), axis=1)
        parity = jnp.sum(jnp.where(is_wanted, offsets[None, :], 0), axis=1) % 2
        compact = jnp.take(landed.reshape(-1, landed.shape[-1]), source * 2 + parity, axis=0)

    def y_send(x, s):
        return lax.ppermute(x, "y", [(i, (i + s) % y_count) for i in range(y_count)])

    row_norm = jnp.einsum("rd,rd->r", pool, pool, preferred_element_type=jnp.float32)

    def core_swap(x):
        return lax.ppermute(x, "c", [(0, 1), (1, 0)])

    with jax.named_scope("spread_centers"):
        plane = replicate_gather(compact, ("z", "x"), z_count * x_count)
        y_near = y_send(plane, 1), y_send(plane, -1)
        split = plane.shape[0] // 2
        y_far = jnp.concatenate(
            [y_send(y_near[0][:split], 1), y_send(y_near[1][split:], -1)], axis=0
        )
        pieces = [plane, core_swap(plane)]
        for part in y_near:
            pieces += [part, core_swap(part)]
        pieces += [y_far, core_swap(y_far)]

    with jax.named_scope("distance_min"):
        running = nearest
        for piece in pieces:
            running = fold_chunk(pool, row_norm, running, piece)
    return running


def solution(mesh):
    grp_count = mesh.shape["grp"]
    dev_count = mesh.shape["dev"]
    y_count = dev_count // (X_CHIPS * CORES)
    torus = Mesh(mesh.devices.reshape(grp_count, y_count, X_CHIPS, CORES), ("z",) + DEV_AXES)
    rows = ("z",) + DEV_AXES
    in_specs = (P(rows, None), P(rows), P("z", None), P("z", None))
    out_specs = P(rows)
    return jax.shard_map(shards, mesh=torus, in_specs=in_specs, out_specs=out_specs, check_vma=False)
```

```python
import math

import jax
import jax.numpy as jnp
from jax import lax
from jax.experimental import pallas as pl
from jax.experimental.pallas import tpu as pltpu
from jax.sharding import Mesh, PartitionSpec as P

MOST = 32
X_CHIPS = 4
CORES = 2


def fold_chunk(pool_rows, row_norm, running, fragment):
    center_norm = jnp.einsum("cd,cd->c", fragment, fragment, preferred_element_type=jnp.float32)
    total_rows = pool_rows.shape[0]
    block = total_rows
    blocks = total_rows // block

    def one_block(args):
        block_rows, block_norm, block_near = args
        inner = lax.dot_general(
            block_rows, fragment, (((1,), (1,)), ((), ())), preferred_element_type=jnp.float32
        )
        distance = jnp.maximum(block_norm[:, None] + center_norm[None, :] - 2.0 * inner, 0.0)
        return jnp.minimum(block_near, jnp.min(distance, axis=1))

    result = lax.map(
        one_block,
        (
            pool_rows.reshape(blocks, block, pool_rows.shape[1]),
            row_norm.reshape(blocks, block),
            running.reshape(blocks, block),
        ),
    )
    return result.reshape(total_rows)


def ring_gather(block, send, size):
    got = [block]
    fwd = block
    bwd = block
    for _ in range((size - 1) // 2):
        fwd = send(fwd, 1)
        bwd = send(bwd, -1)
        got += [fwd, bwd]
    if size % 2 == 0:
        fwd = send(fwd, 1)
        got.append(fwd)
    return got


def _gather_rows_kernel(index_ref, table_ref, out_ref, sems):
    count = out_ref.shape[0]

    def copy(r):
        return pltpu.make_async_copy(
            table_ref.at[pl.ds(pl.multiple_of(index_ref[r] * 2, 2), 2)], out_ref.at[r], sems.at[r]
        )

    for r in range(count):
        copy(r).start()
    for r in range(count):
        copy(r).wait()


def gather_rows(table, index):
    count = index.shape[0]
    width = table.shape[1]
    index = jnp.clip(index // 2, 0, table.shape[0] // 2 - 1).astype(jnp.int32)
    return pl.pallas_call(
        _gather_rows_kernel,
        out_shape=jax.ShapeDtypeStruct((count, 2, width), table.dtype),
        in_specs=[pl.BlockSpec(memory_space=pltpu.SMEM), pl.BlockSpec(memory_space=pl.ANY)],
        out_specs=pl.BlockSpec(memory_space=pltpu.VMEM),
        scratch_shapes=[pltpu.SemaphoreType.DMA((count,))],
        cost_estimate=pl.CostEstimate(
            flops=0, bytes_accessed=2 * count * width * table.dtype.itemsize, transcendentals=0
        ),
    )(index, table)


def replicate_gather(x, axes, count):
    copies = jnp.broadcast_to(x[None], (count,) + x.shape)
    got = lax.all_to_all(copies, axes, 0, 0, tiled=True)
    return got.reshape((count * x.shape[0],) + x.shape[1:])


DEV_AXES = ("y", "x", "c")


def shards(pool, nearest, center_owner, center_offset):
    owners = center_owner[0]
    offsets = center_offset[0]
    dev_count = lax.axis_size(DEV_AXES)
    z_count = lax.axis_size("z")
    x_count = lax.axis_size("x")
    y_count = lax.axis_size("y")
    my_index = lax.axis_index(DEV_AXES)
    per_device = owners.shape[0] // dev_count

    with jax.named_scope("compact_centers"):
        devices = jnp.arange(dev_count, dtype=jnp.int32)
        center_count = owners.shape[0]
        order = lax.broadcasted_iota(jnp.int32, (center_count, center_count), 1) < lax.broadcasted_iota(
            jnp.int32, (center_count, center_count), 0
        )
        before = (owners[None, :] < owners[:, None]) | (
            (owners[None, :] == owners[:, None]) & order
        )
        position = jnp.sum(before.astype(jnp.int32), axis=1)
        to_peer = ((owners == my_index)[None, :]) & (
            (position % dev_count)[None, :] == devices[:, None]
        )
        peer_offset = jnp.sum(jnp.where(to_peer, offsets[None, :], 0), axis=1)
        send_rows = gather_rows(pool, peer_offset)
        landed = lax.all_to_all(send_rows, DEV_AXES, 0, 0, tiled=True)
        wanted = my_index + dev_count * jnp.arange(per_device, dtype=jnp.int32)
        is_wanted = position[None, :] == wanted[:, None]
        source = jnp.sum(jnp.where(is_wanted, owners[None, :], 0), axis=1)
        parity = jnp.sum(jnp.where(is_wanted, offsets[None, :], 0), axis=1) % 2
        compact = jnp.take(landed.reshape(-1, landed.shape[-1]), source * 2 + parity, axis=0)

    def y_send(x, s):
        return lax.ppermute(x, "y", [(i, (i + s) % y_count) for i in range(y_count)])

    row_norm = jnp.einsum("rd,rd->r", pool, pool, preferred_element_type=jnp.float32)

    def core_swap(x):
        return lax.ppermute(x, "c", [(0, 1), (1, 0)])

    with jax.named_scope("spread_centers"):
        plane = replicate_gather(compact, ("x", "z"), z_count * x_count)
        y_near = y_send(plane, 1), y_send(plane, -1)
        split = plane.shape[0] // 2
        y_far = jnp.concatenate(
            [y_send(y_near[0][:split], 1), y_send(y_near[1][split:], -1)], axis=0
        )
        near = jnp.concatenate(y_near, axis=0)
        pieces = [plane, core_swap(plane), near, core_swap(near), y_far, core_swap(y_far)]

    with jax.named_scope("distance_min"):
        running = nearest
        for piece in pieces:
            running = fold_chunk(pool, row_norm, running, piece)
    return running


def solution(mesh):
    grp_count = mesh.shape["grp"]
    dev_count = mesh.shape["dev"]
    y_count = dev_count // (X_CHIPS * CORES)
    torus = Mesh(mesh.devices.reshape(grp_count, y_count, X_CHIPS, CORES), ("z",) + DEV_AXES)
    rows = ("z",) + DEV_AXES
    in_specs = (P(rows, None), P(rows), P("z", None), P("z", None))
    out_specs = P(rows)
    return jax.shard_map(shards, mesh=torus, in_specs=in_specs, out_specs=out_specs, check_vma=False)
```

```python
import math

import jax
import jax.numpy as jnp
from jax import lax
from jax.experimental import pallas as pl
from jax.experimental.pallas import tpu as pltpu
from jax.sharding import Mesh, PartitionSpec as P

MOST = 32
X_CHIPS = 4
CORES = 2


def fold_chunk(pool_rows, row_norm, running, fragment):
    center_norm = jnp.einsum("cd,cd->c", fragment, fragment, preferred_element_type=jnp.float32)
    total_rows = pool_rows.shape[0]
    block = total_rows
    blocks = total_rows // block

    def one_block(args):
        block_rows, block_norm, block_near = args
        inner = lax.dot_general(
            block_rows, fragment, (((1,), (1,)), ((), ())), preferred_element_type=jnp.float32
        )
        distance = jnp.maximum(block_norm[:, None] + center_norm[None, :] - 2.0 * inner, 0.0)
        return jnp.minimum(block_near, jnp.min(distance, axis=1))

    result = lax.map(
        one_block,
        (
            pool_rows.reshape(blocks, block, pool_rows.shape[1]),
            row_norm.reshape(blocks, block),
            running.reshape(blocks, block),
        ),
    )
    return result.reshape(total_rows)


def ring_gather(block, send, size):
    got = [block]
    fwd = block
    bwd = block
    for _ in range((size - 1) // 2):
        fwd = send(fwd, 1)
        bwd = send(bwd, -1)
        got += [fwd, bwd]
    if size % 2 == 0:
        fwd = send(fwd, 1)
        got.append(fwd)
    return got


def _gather_rows_kernel(index_ref, table_ref, out_ref, sems):
    count = out_ref.shape[0]

    def copy(r):
        return pltpu.make_async_copy(
            table_ref.at[pl.ds(pl.multiple_of(index_ref[r] * 2, 2), 2)], out_ref.at[r], sems.at[r]
        )

    for r in range(count):
        copy(r).start()
    for r in range(count):
        copy(r).wait()


def gather_rows(table, index):
    count = index.shape[0]
    width = table.shape[1]
    index = jnp.clip(index // 2, 0, table.shape[0] // 2 - 1).astype(jnp.int32)
    return pl.pallas_call(
        _gather_rows_kernel,
        out_shape=jax.ShapeDtypeStruct((count, 2, width), table.dtype),
        in_specs=[pl.BlockSpec(memory_space=pltpu.SMEM), pl.BlockSpec(memory_space=pl.ANY)],
        out_specs=pl.BlockSpec(memory_space=pltpu.VMEM),
        scratch_shapes=[pltpu.SemaphoreType.DMA((count,))],
        cost_estimate=pl.CostEstimate(
            flops=0, bytes_accessed=2 * count * width * table.dtype.itemsize, transcendentals=0
        ),
    )(index, table)


def replicate_gather(x, axes, count):
    copies = jnp.broadcast_to(x[None], (count,) + x.shape)
    got = lax.all_to_all(copies, axes, 0, 0, tiled=True)
    return got.reshape((count * x.shape[0],) + x.shape[1:])


DEV_AXES = ("y", "x", "c")


def shards(pool, nearest, center_owner, center_offset):
    owners = center_owner[0]
    offsets = center_offset[0]
    dev_count = lax.axis_size(DEV_AXES)
    z_count = lax.axis_size("z")
    x_count = lax.axis_size("x")
    y_count = lax.axis_size("y")
    my_index = lax.axis_index(DEV_AXES)
    per_device = owners.shape[0] // dev_count

    with jax.named_scope("compact_centers"):
        devices = jnp.arange(dev_count, dtype=jnp.int32)
        center_count = owners.shape[0]
        order = lax.broadcasted_iota(jnp.int32, (center_count, center_count), 1) < lax.broadcasted_iota(
            jnp.int32, (center_count, center_count), 0
        )
        before = (owners[None, :] < owners[:, None]) | (
            (owners[None, :] == owners[:, None]) & order
        )
        position = jnp.sum(before.astype(jnp.int32), axis=1)
        to_peer = ((owners == my_index)[None, :]) & (
            (position % dev_count)[None, :] == devices[:, None]
        )
        peer_offset = jnp.sum(jnp.where(to_peer, offsets[None, :], 0), axis=1)
        send_rows = gather_rows(pool, peer_offset)
        grid = (y_count, x_count, dev_count // (y_count * x_count))
        tail = send_rows.shape[1:]
        flip = (2, 1, 0) + tuple(range(3, 3 + len(tail)))
        reordered = send_rows.reshape(grid + tail).transpose(flip).reshape(send_rows.shape)
        landed = lax.all_to_all(reordered, DEV_AXES[::-1], 0, 0, tiled=True)
        landed = landed.reshape(grid[::-1] + tail).transpose(flip).reshape(send_rows.shape)
        wanted = my_index + dev_count * jnp.arange(per_device, dtype=jnp.int32)
        is_wanted = position[None, :] == wanted[:, None]
        source = jnp.sum(jnp.where(is_wanted, owners[None, :], 0), axis=1)
        parity = jnp.sum(jnp.where(is_wanted, offsets[None, :], 0), axis=1) % 2
        compact = jnp.take(landed.reshape(-1, landed.shape[-1]), source * 2 + parity, axis=0)

    def y_send(x, s):
        return lax.ppermute(x, "y", [(i, (i + s) % y_count) for i in range(y_count)])

    row_norm = jnp.einsum("rd,rd->r", pool, pool, preferred_element_type=jnp.float32)

    def core_swap(x):
        return lax.ppermute(x, "c", [(0, 1), (1, 0)])

    with jax.named_scope("spread_centers"):
        plane = replicate_gather(compact, ("x", "z"), z_count * x_count)
        y_near = y_send(plane, 1), y_send(plane, -1)
        split = plane.shape[0] // 2
        y_far = jnp.concatenate(
            [y_send(y_near[0][:split], 1), y_send(y_near[1][split:], -1)], axis=0
        )
        near = jnp.concatenate(y_near, axis=0)
        pieces = [plane, core_swap(plane), near, core_swap(near), y_far, core_swap(y_far)]

    with jax.named_scope("distance_min"):
        running = nearest
        for piece in pieces:
            running = fold_chunk(pool, row_norm, running, piece)
    return running


def solution(mesh):
    grp_count = mesh.shape["grp"]
    dev_count = mesh.shape["dev"]
    y_count = dev_count // (X_CHIPS * CORES)
    torus = Mesh(mesh.devices.reshape(grp_count, y_count, X_CHIPS, CORES), ("z",) + DEV_AXES)
    rows = ("z",) + DEV_AXES
    in_specs = (P(rows, None), P(rows), P("z", None), P("z", None))
    out_specs = P(rows)
    return jax.shard_map(shards, mesh=torus, in_specs=in_specs, out_specs=out_specs, check_vma=False)
```

```python
import math

import jax
import jax.numpy as jnp
from jax import lax
from jax.experimental import pallas as pl
from jax.experimental.pallas import tpu as pltpu
from jax.sharding import Mesh, PartitionSpec as P

MOST = 32
X_CHIPS = 4
CORES = 2


def fold_chunk(pool_rows, row_norm, running, fragment):
    center_norm = jnp.einsum("cd,cd->c", fragment, fragment, preferred_element_type=jnp.float32)
    total_rows = pool_rows.shape[0]
    block = total_rows
    blocks = total_rows // block

    def one_block(args):
        block_rows, block_norm, block_near = args
        inner = lax.dot_general(
            block_rows, fragment, (((1,), (1,)), ((), ())), preferred_element_type=jnp.float32
        )
        distance = jnp.maximum(block_norm[:, None] + center_norm[None, :] - 2.0 * inner, 0.0)
        return jnp.minimum(block_near, jnp.min(distance, axis=1))

    result = lax.map(
        one_block,
        (
            pool_rows.reshape(blocks, block, pool_rows.shape[1]),
            row_norm.reshape(blocks, block),
            running.reshape(blocks, block),
        ),
    )
    return result.reshape(total_rows)


def ring_gather(block, send, size):
    got = [block]
    fwd = block
    bwd = block
    for _ in range((size - 1) // 2):
        fwd = send(fwd, 1)
        bwd = send(bwd, -1)
        got += [fwd, bwd]
    if size % 2 == 0:
        fwd = send(fwd, 1)
        got.append(fwd)
    return got


def _gather_rows_kernel(index_ref, table_ref, out_ref, sems):
    count = out_ref.shape[0]

    def copy(r):
        return pltpu.make_async_copy(
            table_ref.at[pl.ds(pl.multiple_of(index_ref[r] * 2, 2), 2)], out_ref.at[r], sems.at[r]
        )

    for r in range(count):
        copy(r).start()
    for r in range(count):
        copy(r).wait()


def gather_rows(table, index):
    count = index.shape[0]
    width = table.shape[1]
    index = jnp.clip(index // 2, 0, table.shape[0] // 2 - 1).astype(jnp.int32)
    return pl.pallas_call(
        _gather_rows_kernel,
        out_shape=jax.ShapeDtypeStruct((count, 2, width), table.dtype),
        in_specs=[pl.BlockSpec(memory_space=pltpu.SMEM), pl.BlockSpec(memory_space=pl.ANY)],
        out_specs=pl.BlockSpec(memory_space=pltpu.VMEM),
        scratch_shapes=[pltpu.SemaphoreType.DMA((count,))],
        cost_estimate=pl.CostEstimate(
            flops=0, bytes_accessed=2 * count * width * table.dtype.itemsize, transcendentals=0
        ),
    )(index, table)


def replicate_gather(x, axes, count):
    copies = jnp.broadcast_to(x[None], (count,) + x.shape)
    got = lax.all_to_all(copies, axes, 0, 0, tiled=True)
    return got.reshape((count * x.shape[0],) + x.shape[1:])


DEV_AXES = ("y", "x", "c")


def shards(pool, nearest, center_owner, center_offset):
    owners = center_owner[0]
    offsets = center_offset[0]
    dev_count = lax.axis_size(DEV_AXES)
    z_count = lax.axis_size("z")
    x_count = lax.axis_size("x")
    y_count = lax.axis_size("y")
    my_index = lax.axis_index(DEV_AXES)
    per_device = owners.shape[0] // dev_count

    with jax.named_scope("compact_centers"):
        devices = jnp.arange(dev_count, dtype=jnp.int32)
        center_count = owners.shape[0]
        order = lax.broadcasted_iota(jnp.int32, (center_count, center_count), 1) < lax.broadcasted_iota(
            jnp.int32, (center_count, center_count), 0
        )
        before = (owners[None, :] < owners[:, None]) | (
            (owners[None, :] == owners[:, None]) & order
        )
        position = jnp.sum(before.astype(jnp.int32), axis=1)
        to_peer = ((owners == my_index)[None, :]) & (
            (position % dev_count)[None, :] == devices[:, None]
        )
        peer_offset = jnp.sum(jnp.where(to_peer, offsets[None, :], 0), axis=1)
        send_rows = gather_rows(pool, peer_offset)
        peer_axes = DEV_AXES[::-1]
        landed = lax.all_to_all(send_rows, peer_axes, 0, 0, tiled=True)
        wanted = lax.axis_index(peer_axes) + dev_count * jnp.arange(per_device, dtype=jnp.int32)
        is_wanted = position[None, :] == wanted[:, None]
        source = jnp.sum(jnp.where(is_wanted, owners[None, :], 0), axis=1)
        parity = jnp.sum(jnp.where(is_wanted, offsets[None, :], 0), axis=1) % 2
        cores = dev_count // (y_count * x_count)
        source_peer = ((source % cores) * x_count + (source // cores) % x_count) * y_count + source // (
            cores * x_count
        )
        compact = jnp.take(landed.reshape(-1, landed.shape[-1]), source_peer * 2 + parity, axis=0)

    def y_send(x, s):
        return lax.ppermute(x, "y", [(i, (i + s) % y_count) for i in range(y_count)])

    row_norm = jnp.einsum("rd,rd->r", pool, pool, preferred_element_type=jnp.float32)

    def core_swap(x):
        return lax.ppermute(x, "c", [(0, 1), (1, 0)])

    with jax.named_scope("spread_centers"):
        plane = replicate_gather(compact, ("x", "z"), z_count * x_count)
        y_near = y_send(plane, 1), y_send(plane, -1)
        split = plane.shape[0] // 2
        y_far = jnp.concatenate(
            [y_send(y_near[0][:split], 1), y_send(y_near[1][split:], -1)], axis=0
        )
        near = jnp.concatenate(y_near, axis=0)
        pieces = [plane, core_swap(plane), near, core_swap(near), y_far, core_swap(y_far)]

    with jax.named_scope("distance_min"):
        running = nearest
        for piece in pieces:
            running = fold_chunk(pool, row_norm, running, piece)
    return running


def solution(mesh):
    grp_count = mesh.shape["grp"]
    dev_count = mesh.shape["dev"]
    y_count = dev_count // (X_CHIPS * CORES)
    torus = Mesh(mesh.devices.reshape(grp_count, y_count, X_CHIPS, CORES), ("z",) + DEV_AXES)
    rows = ("z",) + DEV_AXES
    in_specs = (P(rows, None), P(rows), P("z", None), P("z", None))
    out_specs = P(rows)
    return jax.shard_map(shards, mesh=torus, in_specs=in_specs, out_specs=out_specs, check_vma=False)
```
